128 devices in a mesh: amp: 64 (over x, z, y_hi, core), grp: 2 (over y_lo).
Axes of the slice: x: 4, y: 4 (y_hi: 2, y_lo: 2; y = y_hi * 2 + y_lo), z: 4, core: 2. Of those that a mesh axis runs over, the one named last changes fastest.
Arguments:
- amplitudes: bfloat16 [16384, 128, 128], P(('amp', 'grp')), may hold values from -6 to 6
- adjoint: bfloat16 [16384, 128, 128], P(('amp', 'grp')), may hold values from -6 to 6
- gate_mats: bfloat16 [20, 128, 128], replicated, as said below
- gate_order: int32 [20], replicated, may hold values from 0 to 19, each once
- gate_window: int32 [20], replicated, may hold values from 0 to 1
- swap_window: int32 [3], replicated, may hold values from 0 to 1
Outputs:
- final_state: bfloat16 [16384, 128, 128], P(('amp', 'grp'))
- environment: float32 [512, 512], P('grp')
The draws below stay inside these ranges and needn't reach their ends.
Inputs may be any that keep to these rules, and one draw needn't show every extreme that they name: `gate_mats`: each gate matrix is an orthogonal matrix rounded to bfloat16.
All inputs are finite; a program needn't handle non-finite values.
Results may differ from the reference program's by a relative error of at most 0.04.
Values may be sent and summed in bfloat16 or wider, within the bound.
No kernel may reach another device: no remote copies, remote signals or barrier semaphores. Data moves between devices by JAX's collectives and lax.ppermute only.
A program may use at most 128 MiB of HBM per device.

```python
import math
import jax
import jax.numpy as jnp
from jax import lax

WIN = 128
SLAB = 128
SEGS = 4
GATES = 5
NG = 20
SWAPS = 3
AMPS = 64
GROUPS = 2
ROWS = 16384
ENV = 512


def one_orthogonal(key):
    key_rows, key_cols, key_signs, key_flips = jax.random.split(key, 4)
    row_perm = jax.random.permutation(key_rows, WIN).astype(jnp.int32)
    col_perm = jax.random.permutation(key_cols, WIN).astype(jnp.int32)
    row_signs = (2 * jax.random.randint(key_signs, (WIN,), 0, 2) - 1).astype(jnp.float32)
    col_signs = (2 * jax.random.randint(key_flips, (WIN,), 0, 2) - 1).astype(jnp.float32)
    phase = (2 * row_perm[:, None] + 1) * (2 * col_perm[None, :] + 1) % (4 * WIN)
    angle = phase.astype(jnp.float32) * jnp.float32(math.pi / (2 * WIN))
    table = jnp.cos(angle) * jnp.float32(math.sqrt(2.0 / WIN))
    return row_signs[:, None] * table * col_signs[None, :]


def draw_gate_mats(key, part):
    keys = jax.random.split(jax.random.fold_in(key, 71), NG)
    return jax.vmap(one_orthogonal)(keys).astype(jnp.bfloat16)


def with_ends(drawn, own_key, least, high):
    spot = [jax.random.randint(jax.random.fold_in(own_key, axis), (), 0, length) for axis, length in enumerate(drawn.shape)]
    main_axis = drawn.shape.index(max(drawn.shape))
    beside = spot[:main_axis] + [(spot[main_axis] + 1) % drawn.shape[main_axis]] + spot[main_axis + 1:]
    return drawn.at[tuple(spot)].set(least).at[tuple(beside)].set(high)


def levels(stream_key, extent, pieces, smallest, largest):
    loudness, own = 1.0, jax.random.fold_in(stream_key, 6)
    for dim, shards_of in pieces:
        steps = jnp.exp(jax.random.uniform(jax.random.fold_in(own, dim), (shards_of,), jnp.float32, smallest / len(pieces), largest / len(pieces)))
        loudness = loudness * jnp.repeat(steps, extent[dim] // shards_of).reshape([-1 if axis == dim else 1 for axis in range(len(extent))])
    return loudness


def scatter_about(rng, extent, scale, limit, cuts=(), held_as=jnp.bfloat16):
    result = scale * jax.random.normal(rng, extent, jnp.float32)
    if cuts:
        result = result * levels(rng, extent, cuts, -0.22, 0.18)
    return jnp.clip(result, -limit, limit).astype(held_as)


def setup_inputs(seed: int = 0) -> dict:
    key_list = jax.random.split(jax.random.key(seed), 7)
    return {
        "amplitudes": scatter_about(key_list[0], (ROWS, WIN, WIN), 1.0, 6.0, ((0, 128),)),
        "adjoint": scatter_about(key_list[1], (ROWS, WIN, WIN), 1.0, 6.0, ((0, 128),)),
        "gate_mats": draw_gate_mats(jax.random.fold_in(key_list[6], 71), 0),
        "gate_order": jax.random.permutation(key_list[3], NG).astype(jnp.int32),
        "gate_window": with_ends(jax.random.randint(key_list[4], (NG,), 0, 2), jax.random.fold_in(key_list[4], 1), 0, 1).astype(jnp.int32),
        "swap_window": jax.random.randint(key_list[5], (SWAPS,), 0, 2).astype(jnp.int32),
    }


def apply_gate(values, matrix, window):
    wide = matrix.astype(jnp.float32)

    def on_last(current):
        return jnp.einsum('rab,cb->rac', current.astype(jnp.float32), wide).astype(jnp.bfloat16)

    def on_middle(current):
        return jnp.einsum('rab,ca->rcb', current.astype(jnp.float32), wide).astype(jnp.bfloat16)
    return lax.switch(window, [on_last, on_middle], values)

def swap_qubits(values, window):
    inner_size = WIN // AMPS

    def on_last(current):
        shaped = current.reshape(AMPS, GROUPS * SLAB, WIN, AMPS, inner_size)
        return jnp.swapaxes(shaped, 0, 3).reshape(ROWS, WIN, WIN)

    def on_middle(current):
        shaped = current.reshape(AMPS, GROUPS * SLAB, AMPS, inner_size, WIN)
        return jnp.swapaxes(shaped, 0, 2).reshape(ROWS, WIN, WIN)
    return lax.switch(window, [on_last, on_middle], values)

def reference(amplitudes, adjoint, gate_mats, gate_order, gate_window, swap_window):
    current = amplitudes
    for segment in range(SEGS):

        def one_gate(position, values):
            index = segment * GATES + position
            return apply_gate(values, gate_mats[gate_order[index]], gate_window[index])
        current = lax.fori_loop(0, GATES, one_gate, current)
        if segment < SEGS - 1:
            current = swap_qubits(current, swap_window[segment])
    final_state = current
    flattened = final_state.reshape(ROWS * WIN // 4, ENV)
    adjoint_flat = adjoint.reshape(ROWS * WIN // 4, ENV)
    correlation = lax.dot_general(adjoint_flat, flattened, (((0,), (0,)), ((), ())), preferred_element_type=jnp.float32)
    gram = lax.dot_general(correlation, correlation, (((0,), (0,)), ((), ())), precision=lax.Precision.HIGHEST, preferred_element_type=jnp.float32)
    scale = 1.0 / jnp.sqrt(jnp.trace(gram) / ENV + 1e-06)
    product = jnp.dot(correlation, gram, precision=lax.Precision.HIGHEST)
    environment = jnp.sqrt(jnp.float32(ENV)) * (1.5 * scale * correlation - 0.5 * scale * scale * scale * product)
    return (final_state, environment)
```

```python
import jax
import jax.numpy as jnp
from jax import lax
from jax.experimental import pallas as pl
from jax.experimental.pallas import tpu as pltpu
from jax.sharding import PartitionSpec as P

SEGS = 4
GATES = 5
BLOCK = 16


def make_kernel(slab_in, slab_out):
    def kernel(order_ref, major_ref, flip_ref, gates_ref, x_ref, o_ref, held):
        wide, block, _ = held.shape[0] // BLOCK, BLOCK, None
        rows = pl.ds

        def slab_rows(s):
            return rows(s, wide, stride=block)

        if slab_in:
            for s in range(block):
                held[slab_rows(s), :] = x_ref[s].astype(jnp.float32)
        else:
            held[...] = x_ref[...].astype(jnp.float32).reshape(wide * block, -1)

        for position in range(GATES):
            matrix = gates_ref[order_ref[position]]

            @pl.when(major_ref[position] == 1)
            def _(matrix=matrix):
                def body(s, carry):
                    tile = held[slab_rows(s), :].astype(jnp.bfloat16)
                    out = jnp.dot(matrix, tile, preferred_element_type=jnp.float32)
                    held[slab_rows(s), :] = out.astype(jnp.bfloat16).astype(jnp.float32)
                    return carry

                lax.fori_loop(0, block, body, 0)

            @pl.when(major_ref[position] == 0)
            def _(matrix=matrix):
                flat = held[...].astype(jnp.bfloat16)
                out = lax.dot_general(
                    flat, matrix, (((1,), (1,)), ((), ())), preferred_element_type=jnp.float32
                )
                held[...] = out.astype(jnp.bfloat16).astype(jnp.float32)

        @pl.when(flip_ref[0] == 1)
        def _():
            def body(s, carry):
                held[slab_rows(s), :] = held[slab_rows(s), :].T
                return carry

            lax.fori_loop(0, block, body, 0)

        if slab_out:
            for s in range(block):
                o_ref[s] = held[slab_rows(s), :].astype(jnp.bfloat16)
        else:
            o_ref[...] = held[...].astype(jnp.bfloat16).reshape(o_ref.shape)

    return kernel


def run_segment(values, gate_mats, order, major, flip, slab_in, slab_out):
    wide = gate_mats.shape[1]
    slabs = values.shape[0] if slab_in else values.shape[1]
    lanes = values.shape[2]
    slab_spec = pl.BlockSpec((BLOCK, wide, lanes), lambda i, o, m, f: (i, 0, 0))
    major_spec = pl.BlockSpec((wide, BLOCK, lanes), lambda i, o, m, f: (0, i, 0))
    out_shape = (slabs, wide, lanes) if slab_out else (wide, slabs, lanes)
    grid_spec = pltpu.PrefetchScalarGridSpec(
        num_scalar_prefetch=3,
        grid=(slabs // BLOCK,),
        in_specs=[
            pl.BlockSpec(gate_mats.shape, lambda i, o, m, f: (0, 0, 0)),
            slab_spec if slab_in else major_spec,
        ],
        out_specs=slab_spec if slab_out else major_spec,
        scratch_shapes=[pltpu.VMEM((wide * BLOCK, lanes), jnp.float32)],
    )
    return pl.pallas_call(
        make_kernel(slab_in, slab_out),
        grid_spec=grid_spec,
        out_shape=jax.ShapeDtypeStruct(out_shape, values.dtype),
        compiler_params=pltpu.CompilerParams(dimension_semantics=("arbitrary",)),
    )(order, major, flip, gate_mats, values)


def swap_major(values):
    amp_count = lax.axis_size("amp")
    wide, slabs, lanes = values.shape
    split = values.reshape(amp_count, wide // amp_count, slabs, lanes)
    swapped = lax.all_to_all(split, "amp", split_axis=0, concat_axis=0, tiled=True)
    return swapped.reshape(wide, slabs, lanes)


def on_device(amplitudes, adjoint, gate_mats, gate_order, gate_window, swap_window):
    current = amplitudes
    lanes_window = jnp.int32(0)
    for segment in range(SEGS):
        order = lax.dynamic_slice_in_dim(gate_order, segment * GATES, GATES)
        window = lax.dynamic_slice_in_dim(gate_window, segment * GATES, GATES)
        major = (window != lanes_window).astype(jnp.int32)
        if segment < SEGS - 1:
            flip = (swap_window[segment] == lanes_window).astype(jnp.int32)
        else:
            flip = (lanes_window != 0).astype(jnp.int32)
        current = run_segment(
            current, gate_mats, order, major, flip.reshape(1),
            slab_in=segment == 0, slab_out=segment == SEGS - 1,
        )
        lanes_window = jnp.where(flip == 1, 1 - lanes_window, lanes_window)
        if segment < SEGS - 1:
            current = swap_major(current)
    order = 4 * amplitudes.shape[2]
    owned_rows = order // lax.axis_size("grp")
    flattened = current.reshape(-1, order)
    adjoint_flat = adjoint.reshape(-1, order)
    partial_correlation = lax.dot_general(
        adjoint_flat, flattened, (((0,), (0,)), ((), ())), preferred_element_type=jnp.float32
    )
    summed = lax.psum(partial_correlation, ("amp", "grp"))
    owned = lax.dynamic_slice_in_dim(summed, lax.axis_index("grp") * owned_rows, owned_rows, 0)
    gram = lax.dot_general(
        summed,
        summed,
        (((0,), (0,)), ((), ())),
        precision=lax.Precision.HIGHEST,
        preferred_element_type=jnp.float32,
    )
    scale = 1.0 / jnp.sqrt(jnp.trace(gram) / order + 1e-06)
    product = jnp.dot(owned, gram, precision=lax.Precision.HIGHEST)
    environment = jnp.sqrt(jnp.float32(order)) * (
        1.5 * scale * owned - 0.5 * scale * scale * scale * product
    )
    return (current, environment)


def solution(mesh):
    in_specs = (P(("amp", "grp"), None, None), P(("amp", "grp"), None, None), P(), P(), P(), P())
    out_specs = (P(("amp", "grp"), None, None), P("grp", None))
    return jax.shard_map(
        on_device, mesh=mesh, in_specs=in_specs, out_specs=out_specs, check_vma=False
    )
```

```python
import jax
import jax.numpy as jnp
from jax import lax
from jax.experimental import pallas as pl
from jax.experimental.pallas import tpu as pltpu
from jax.sharding import PartitionSpec as P

SEGS = 4
GATES = 5
BLOCK = 16


def make_kernel(slab_in, slab_out):
    def kernel(order_ref, major_ref, flip_ref, gates_ref, x_ref, o_ref, held):
        block, wide, lanes = held.shape
        if slab_in:
            held[...] = x_ref[...]
        else:
            held[...] = jnp.swapaxes(x_ref[...], 0, 1)

        for position in range(GATES):
            matrix = gates_ref[order_ref[position]]

            @pl.when(major_ref[position] == 1)
            def _(matrix=matrix):
                def body(s, carry):
                    out = jnp.dot(matrix, held[s], preferred_element_type=jnp.float32)
                    held[s] = out.astype(jnp.bfloat16)
                    return carry

                lax.fori_loop(0, block, body, 0, unroll=4)

            @pl.when(major_ref[position] == 0)
            def _(matrix=matrix):
                flat = held[...].reshape(block * wide, lanes)
                out = lax.dot_general(
                    flat, matrix, (((1,), (1,)), ((), ())), preferred_element_type=jnp.float32
                )
                held[...] = out.astype(jnp.bfloat16).reshape(block, wide, lanes)

        @pl.when(flip_ref[0] == 0)
        def _():
            if slab_out:
                o_ref[...] = held[...]
            else:
                o_ref[...] = jnp.swapaxes(held[...], 0, 1)

        @pl.when(flip_ref[0] == 1)
        def _():
            flipped = jnp.swapaxes(held[...], 1, 2)
            if slab_out:
                o_ref[...] = flipped
            else:
                o_ref[...] = jnp.swapaxes(flipped, 0, 1)

    return kernel


def run_segment(values, gate_mats, order, major, flip, slab_in, slab_out):
    wide = gate_mats.shape[1]
    slabs = values.shape[0] if slab_in else values.shape[1]
    lanes = values.shape[2]
    slab_spec = pl.BlockSpec((BLOCK, wide, lanes), lambda i, o, m, f: (i, 0, 0))
    major_spec = pl.BlockSpec((wide, BLOCK, lanes), lambda i, o, m, f: (0, i, 0))
    out_shape = (slabs, wide, lanes) if slab_out else (wide, slabs, lanes)
    grid_spec = pltpu.PrefetchScalarGridSpec(
        num_scalar_prefetch=3,
        grid=(slabs // BLOCK,),
        in_specs=[
            pl.BlockSpec(gate_mats.shape, lambda i, o, m, f: (0, 0, 0)),
            slab_spec if slab_in else major_spec,
        ],
        out_specs=slab_spec if slab_out else major_spec,
        scratch_shapes=[pltpu.VMEM((BLOCK, wide, lanes), jnp.bfloat16)],
    )
    return pl.pallas_call(
        make_kernel(slab_in, slab_out),
        grid_spec=grid_spec,
        out_shape=jax.ShapeDtypeStruct(out_shape, values.dtype),
        compiler_params=pltpu.CompilerParams(dimension_semantics=("arbitrary",)),
    )(order, major, flip, gate_mats, values)


def swap_major(values):
    amp_count = lax.axis_size("amp")
    wide, slabs, lanes = values.shape
    split = values.reshape(amp_count, wide // amp_count, slabs, lanes)
    swapped = lax.all_to_all(split, "amp", split_axis=0, concat_axis=0, tiled=True)
    return swapped.reshape(wide, slabs, lanes)


def all_sum(values, axes):
    count = lax.axis_size(axes)
    pieces = values.reshape(count, -1)
    gathered = lax.all_to_all(pieces, axes, split_axis=0, concat_axis=0, tiled=True)
    reduced = jnp.sum(gathered, axis=0, keepdims=True)
    spread = jnp.broadcast_to(reduced, pieces.shape)
    whole = lax.all_to_all(spread, axes, split_axis=0, concat_axis=0, tiled=True)
    return whole.reshape(values.shape)


def on_device(amplitudes, adjoint, gate_mats, gate_order, gate_window, swap_window):
    current = amplitudes
    lanes_window = jnp.int32(0)
    for segment in range(SEGS):
        order = lax.dynamic_slice_in_dim(gate_order, segment * GATES, GATES)
        window = lax.dynamic_slice_in_dim(gate_window, segment * GATES, GATES)
        major = (window != lanes_window).astype(jnp.int32)
        if segment < SEGS - 1:
            flip = (swap_window[segment] == lanes_window).astype(jnp.int32)
        else:
            flip = (lanes_window != 0).astype(jnp.int32)
        current = run_segment(
            current, gate_mats, order, major, flip.reshape(1),
            slab_in=segment == 0, slab_out=segment == SEGS - 1,
        )
        lanes_window = jnp.where(flip == 1, 1 - lanes_window, lanes_window)
        if segment < SEGS - 1:
            current = swap_major(current)
    order = 4 * amplitudes.shape[2]
    owned_rows = order // lax.axis_size("grp")
    flattened = current.reshape(-1, order)
    adjoint_flat = adjoint.reshape(-1, order)
    partial_correlation = lax.dot_general(
        adjoint_flat, flattened, (((0,), (0,)), ((), ())), preferred_element_type=jnp.float32
    )
    summed = all_sum(partial_correlation, ("amp", "grp"))
    owned = lax.dynamic_slice_in_dim(summed, lax.axis_index("grp") * owned_rows, owned_rows, 0)
    gram = lax.dot_general(
        summed,
        summed,
        (((0,), (0,)), ((), ())),
        precision=lax.Precision.HIGHEST,
        preferred_element_type=jnp.float32,
    )
    scale = 1.0 / jnp.sqrt(jnp.trace(gram) / order + 1e-06)
    product = jnp.dot(owned, gram, precision=lax.Precision.HIGHEST)
    environment = jnp.sqrt(jnp.float32(order)) * (
        1.5 * scale * owned - 0.5 * scale * scale * scale * product
    )
    return (current, environment)


def solution(mesh):
    in_specs = (P(("amp", "grp"), None, None), P(("amp", "grp"), None, None), P(), P(), P(), P())
    out_specs = (P(("amp", "grp"), None, None), P("grp", None))
    return jax.shard_map(
        on_device, mesh=mesh, in_specs=in_specs, out_specs=out_specs, check_vma=False
    )
```

```python
import jax
import jax.numpy as jnp
from jax import lax
from jax.experimental import pallas as pl
from jax.experimental.pallas import tpu as pltpu
from jax.sharding import PartitionSpec as P

SEGS = 4
GATES = 5
BLOCK = 32


def make_kernel(slab_in, slab_out):
    def kernel(order_ref, flip_ref, gates_ref, x_ref, o_ref, held):
        half, wide, pair = held.shape
        lanes = pair // 2
        if slab_in:
            slabs = x_ref[...]
        else:
            slabs = jnp.swapaxes(x_ref[...], 0, 1)
        held[:, :, :lanes] = slabs[:half]
        held[:, :, lanes:] = slabs[half:]

        def flip():
            held[:, :, :lanes] = jnp.swapaxes(held[:, :, :lanes], 1, 2)
            held[:, :, lanes:] = jnp.swapaxes(held[:, :, lanes:], 1, 2)

        def one_gate(position, carry):
            pl.when(flip_ref[position] == 1)(flip)
            matrix = gates_ref[order_ref[position]]
            flat = held[...].reshape(half * wide, pair)
            out = jnp.dot(flat, matrix, preferred_element_type=jnp.float32)
            held[...] = out.astype(jnp.bfloat16).reshape(half, wide, pair)
            return carry

        lax.fori_loop(0, GATES, one_gate, 0)
        pl.when(flip_ref[GATES] == 1)(flip)

        first = held[:, :, :lanes]
        second = held[:, :, lanes:]
        if slab_out:
            o_ref[:half] = first
            o_ref[half:] = second
        else:
            o_ref[:, :half, :] = jnp.swapaxes(first, 0, 1)
            o_ref[:, half:, :] = jnp.swapaxes(second, 0, 1)

    return kernel


def block_diagonal(gate_mats):
    transposed = jnp.swapaxes(gate_mats, 1, 2)
    zeros = jnp.zeros_like(transposed)
    top = jnp.concatenate([transposed, zeros], axis=2)
    bottom = jnp.concatenate([zeros, transposed], axis=2)
    return jnp.concatenate([top, bottom], axis=1)


def run_segment(values, gates_bd, order, flips, slab_in, slab_out):
    wide = gates_bd.shape[1] // 2
    slabs = values.shape[0] if slab_in else values.shape[1]
    lanes = values.shape[2]
    slab_spec = pl.BlockSpec((BLOCK, wide, lanes), lambda i, o, f: (i, 0, 0))
    major_spec = pl.BlockSpec((wide, BLOCK, lanes), lambda i, o, f: (0, i, 0))
    out_shape = (slabs, wide, lanes) if slab_out else (wide, slabs, lanes)
    grid_spec = pltpu.PrefetchScalarGridSpec(
        num_scalar_prefetch=2,
        grid=(slabs // BLOCK,),
        in_specs=[
            pl.BlockSpec(gates_bd.shape, lambda i, o, f: (0, 0, 0)),
            slab_spec if slab_in else major_spec,
        ],
        out_specs=slab_spec if slab_out else major_spec,
        scratch_shapes=[pltpu.VMEM((BLOCK // 2, wide, 2 * lanes), jnp.bfloat16)],
    )
    return pl.pallas_call(
        make_kernel(slab_in, slab_out),
        grid_spec=grid_spec,
        out_shape=jax.ShapeDtypeStruct(out_shape, values.dtype),
        compiler_params=pltpu.CompilerParams(dimension_semantics=("arbitrary",)),
    )(order, flips, gates_bd, values)


def swap_major(values):
    amp_count = lax.axis_size("amp")
    wide, slabs, lanes = values.shape
    split = values.reshape(amp_count, wide // amp_count, slabs, lanes)
    swapped = lax.all_to_all(split, "amp", split_axis=0, concat_axis=0, tiled=True)
    return swapped.reshape(wide, slabs, lanes)


def all_sum(values, axes):
    count = lax.axis_size(axes)
    pieces = values.reshape(count, -1)
    gathered = lax.all_to_all(pieces, axes, split_axis=0, concat_axis=0, tiled=True)
    reduced = jnp.sum(gathered, axis=0, keepdims=True)
    spread = jnp.broadcast_to(reduced, pieces.shape)
    whole = lax.all_to_all(spread, axes, split_axis=0, concat_axis=0, tiled=True)
    return whole.reshape(values.shape)


def on_device(amplitudes, adjoint, gate_mats, gate_order, gate_window, swap_window):
    current = amplitudes
    gates_bd = block_diagonal(gate_mats)
    lanes_window = jnp.int32(0)
    for segment in range(SEGS):
        order = lax.dynamic_slice_in_dim(gate_order, segment * GATES, GATES)
        window = lax.dynamic_slice_in_dim(gate_window, segment * GATES, GATES)
        before = jnp.concatenate([lanes_window.reshape(1), window[:-1]])
        wanted = 1 - swap_window[segment] if segment < SEGS - 1 else jnp.int32(0)
        flips = jnp.concatenate([window != before, (window[-1] != wanted).reshape(1)])
        current = run_segment(
            current, gates_bd, order, flips.astype(jnp.int32),
            slab_in=segment == 0, slab_out=segment == SEGS - 1,
        )
        lanes_window = wanted
        if segment < SEGS - 1:
            current = swap_major(current)
    order = 4 * amplitudes.shape[2]
    owned_rows = order // lax.axis_size("grp")
    flattened = current.reshape(-1, order)
    adjoint_flat = adjoint.reshape(-1, order)
    partial_correlation = lax.dot_general(
        adjoint_flat, flattened, (((0,), (0,)), ((), ())), preferred_element_type=jnp.float32
    )
    summed = all_sum(partial_correlation, ("amp", "grp"))
    owned = lax.dynamic_slice_in_dim(summed, lax.axis_index("grp") * owned_rows, owned_rows, 0)
    gram = lax.dot_general(
        summed,
        summed,
        (((0,), (0,)), ((), ())),
        precision=lax.Precision.HIGHEST,
        preferred_element_type=jnp.float32,
    )
    scale = 1.0 / jnp.sqrt(jnp.trace(gram) / order + 1e-06)
    product = jnp.dot(owned, gram, precision=lax.Precision.HIGHEST)
    environment = jnp.sqrt(jnp.float32(order)) * (
        1.5 * scale * owned - 0.5 * scale * scale * scale * product
    )
    return (current, environment)


def solution(mesh):
    in_specs = (P(("amp", "grp"), None, None), P(("amp", "grp"), None, None), P(), P(), P(), P())
    out_specs = (P(("amp", "grp"), None, None), P("grp", None))
    return jax.shard_map(
        on_device, mesh=mesh, in_specs=in_specs, out_specs=out_specs, check_vma=False
    )
```

```python
import jax
import jax.numpy as jnp
from jax import lax
from jax.experimental import pallas as pl
from jax.experimental.pallas import tpu as pltpu
from jax.sharding import PartitionSpec as P

SEGS = 4
GATES = 5
BLOCK = 32


def make_kernel(slab_in, slab_out):
    def kernel(order_ref, flip_ref, gates_ref, x_ref, o_ref, held):
        half, wide, pair = held.shape
        lanes = pair // 2
        if slab_in:
            slabs = x_ref[...]
        else:
            slabs = jnp.swapaxes(x_ref[...], 0, 1)
        held[:, :, :lanes] = slabs[:half]
        held[:, :, lanes:] = slabs[half:]

        def flip():
            held[:, :, :lanes] = jnp.swapaxes(held[:, :, :lanes], 1, 2)
            held[:, :, lanes:] = jnp.swapaxes(held[:, :, lanes:], 1, 2)

        def one_gate(position, carry):
            pl.when(flip_ref[position] == 1)(flip)
            matrix = gates_ref[order_ref[position]]
            flat = held[...].reshape(half * wide, pair)
            out = jnp.dot(flat, matrix, preferred_element_type=jnp.float32)
            held[...] = out.astype(jnp.bfloat16).reshape(half, wide, pair)
            return carry

        lax.fori_loop(0, GATES, one_gate, 0)
        pl.when(flip_ref[GATES] == 1)(flip)

        first = held[:, :, :lanes]
        second = held[:, :, lanes:]
        if slab_out:
            o_ref[:half] = first
            o_ref[half:] = second
        else:
            o_ref[:, :half, :] = jnp.swapaxes(first, 0, 1)
            o_ref[:, half:, :] = jnp.swapaxes(second, 0, 1)

    return kernel


def block_diagonal(gate_mats):
    transposed = jnp.swapaxes(gate_mats, 1, 2)
    zeros = jnp.zeros_like(transposed)
    top = jnp.concatenate([transposed, zeros], axis=2)
    bottom = jnp.concatenate([zeros, transposed], axis=2)
    return jnp.concatenate([top, bottom], axis=1)


def run_segment(values, gates_bd, order, flips, slab_in, slab_out):
    wide = gates_bd.shape[1] // 2
    slabs = values.shape[0] if slab_in else values.shape[1]
    lanes = values.shape[2]
    slab_spec = pl.BlockSpec((BLOCK, wide, lanes), lambda i, o, f: (i, 0, 0))
    major_spec = pl.BlockSpec((wide, BLOCK, lanes), lambda i, o, f: (0, i, 0))
    out_shape = (slabs, wide, lanes) if slab_out else (wide, slabs, lanes)
    grid_spec = pltpu.PrefetchScalarGridSpec(
        num_scalar_prefetch=2,
        grid=(slabs // BLOCK,),
        in_specs=[
            pl.BlockSpec(gates_bd.shape, lambda i, o, f: (0, 0, 0)),
            slab_spec if slab_in else major_spec,
        ],
        out_specs=slab_spec if slab_out else major_spec,
        scratch_shapes=[pltpu.VMEM((BLOCK // 2, wide, 2 * lanes), jnp.bfloat16)],
    )
    return pl.pallas_call(
        make_kernel(slab_in, slab_out),
        grid_spec=grid_spec,
        out_shape=jax.ShapeDtypeStruct(out_shape, values.dtype),
        compiler_params=pltpu.CompilerParams(dimension_semantics=("arbitrary",)),
    )(order, flips, gates_bd, values)


def swap_major(values):
    amp_count = lax.axis_size("amp")
    wide, slabs, lanes = values.shape
    split = values.reshape(amp_count, wide // amp_count, slabs, lanes)
    swapped = lax.all_to_all(split, "amp", split_axis=0, concat_axis=0, tiled=True)
    return swapped.reshape(wide, slabs, lanes)


def all_sum(values, axes):
    count = lax.axis_size(axes)
    pieces = values.reshape(count, -1).astype(jnp.bfloat16)
    gathered = lax.all_to_all(pieces, axes, split_axis=0, concat_axis=0, tiled=True)
    reduced = jnp.sum(gathered.astype(jnp.float32), axis=0, keepdims=True)
    spread = jnp.broadcast_to(reduced.astype(jnp.bfloat16), pieces.shape)
    whole = lax.all_to_all(spread, axes, split_axis=0, concat_axis=0, tiled=True)
    return whole.reshape(values.shape).astype(jnp.float32)


def on_device(amplitudes, adjoint, gate_mats, gate_order, gate_window, swap_window):
    current = amplitudes
    gates_bd = block_diagonal(gate_mats)
    lanes_window = jnp.int32(0)
    for segment in range(SEGS):
        order = lax.dynamic_slice_in_dim(gate_order, segment * GATES, GATES)
        window = lax.dynamic_slice_in_dim(gate_window, segment * GATES, GATES)
        before = jnp.concatenate([lanes_window.reshape(1), window[:-1]])
        wanted = 1 - swap_window[segment] if segment < SEGS - 1 else jnp.int32(0)
        flips = jnp.concatenate([window != before, (window[-1] != wanted).reshape(1)])
        current = run_segment(
            current, gates_bd, order, flips.astype(jnp.int32),
            slab_in=segment == 0, slab_out=segment == SEGS - 1,
        )
        lanes_window = wanted
        if segment < SEGS - 1:
            current = swap_major(current)
    order = 4 * amplitudes.shape[2]
    owned_rows = order // lax.axis_size("grp")
    flattened = current.reshape(-1, order)
    adjoint_flat = adjoint.reshape(-1, order)
    partial_correlation = lax.dot_general(
        adjoint_flat, flattened, (((0,), (0,)), ((), ())), preferred_element_type=jnp.float32
    )
    summed = all_sum(partial_correlation, ("amp", "grp"))
    owned = lax.dynamic_slice_in_dim(summed, lax.axis_index("grp") * owned_rows, owned_rows, 0)
    gram = lax.dot_general(
        summed,
        summed,
        (((0,), (0,)), ((), ())),
        precision=lax.Precision.HIGHEST,
        preferred_element_type=jnp.float32,
    )
    scale = 1.0 / jnp.sqrt(jnp.trace(gram) / order + 1e-06)
    product = jnp.dot(owned, gram, precision=lax.Precision.HIGHEST)
    environment = jnp.sqrt(jnp.float32(order)) * (
        1.5 * scale * owned - 0.5 * scale * scale * scale * product
    )
    return (current, environment)


def solution(mesh):
    in_specs = (P(("amp", "grp"), None, None), P(("amp", "grp"), None, None), P(), P(), P(), P())
    out_specs = (P(("amp", "grp"), None, None), P("grp", None))
    return jax.shard_map(
        on_device, mesh=mesh, in_specs=in_specs, out_specs=out_specs, check_vma=False
    )
```

```python
import jax
import jax.numpy as jnp
from jax import lax
from jax.experimental import pallas as pl
from jax.experimental.pallas import tpu as pltpu
from jax.sharding import PartitionSpec as P

SEGS = 4
GATES = 5
BLOCK = 32
CHUNKS = 2


def make_kernel(slab_in, slab_out, sources, blocks_per_source):
    def kernel(order_ref, flip_ref, gates_ref, *refs):
        x_refs, o_ref, held = refs[:sources], refs[sources], refs[sources + 1]
        half, wide, pair = held.shape
        lanes = pair // 2

        def load(x_ref):
            if slab_in:
                slabs = x_ref[...]
            else:
                slabs = jnp.swapaxes(x_ref[...], 0, 1)
            held[:, :, :lanes] = slabs[:half]
            held[:, :, lanes:] = slabs[half:]

        if sources == 1:
            load(x_refs[0])
        else:
            step = pl.program_id(0)
            for index, x_ref in enumerate(x_refs):
                inside = (step >= index * blocks_per_source) & (step < (index + 1) * blocks_per_source)
                pl.when(inside)(lambda x_ref=x_ref: load(x_ref))

        def flip():
            held[:, :, :lanes] = jnp.swapaxes(held[:, :, :lanes], 1, 2)
            held[:, :, lanes:] = jnp.swapaxes(held[:, :, lanes:], 1, 2)

        def one_gate(position, carry):
            pl.when(flip_ref[position] == 1)(flip)
            matrix = gates_ref[order_ref[position]]
            flat = held[...].reshape(half * wide, pair)
            out = jnp.dot(flat, matrix, preferred_element_type=jnp.float32)
            held[...] = out.astype(jnp.bfloat16).reshape(half, wide, pair)
            return carry

        lax.fori_loop(0, GATES, one_gate, 0)
        pl.when(flip_ref[GATES] == 1)(flip)

        first = held[:, :, :lanes]
        second = held[:, :, lanes:]
        if slab_out:
            o_ref[:half] = first
            o_ref[half:] = second
        else:
            o_ref[:, :half, :] = jnp.swapaxes(first, 0, 1)
            o_ref[:, half:, :] = jnp.swapaxes(second, 0, 1)

    return kernel


def block_diagonal(gate_mats):
    transposed = jnp.swapaxes(gate_mats, 1, 2)
    zeros = jnp.zeros_like(transposed)
    top = jnp.concatenate([transposed, zeros], axis=2)
    bottom = jnp.concatenate([zeros, transposed], axis=2)
    return jnp.concatenate([top, bottom], axis=1)


def run_segment(sources, gates_bd, order, flips, slab_in, slab_out, slabs, offset=0):
    wide = gates_bd.shape[1] // 2
    lanes = sources[0].shape[2]
    blocks = slabs // BLOCK
    per_source = blocks // len(sources)

    def source_spec(index):
        def pick(i, o, f):
            local = jnp.clip(i - index * per_source, 0, per_source - 1) + offset
            return (local, 0, 0) if slab_in else (0, local, 0)

        shape = (BLOCK, wide, lanes) if slab_in else (wide, BLOCK, lanes)
        return pl.BlockSpec(shape, pick)

    if slab_out:
        out_spec = pl.BlockSpec((BLOCK, wide, lanes), lambda i, o, f: (i, 0, 0))
        out_shape = (slabs, wide, lanes)
    else:
        out_spec = pl.BlockSpec((wide, BLOCK, lanes), lambda i, o, f: (0, i, 0))
        out_shape = (wide, slabs, lanes)
    grid_spec = pltpu.PrefetchScalarGridSpec(
        num_scalar_prefetch=2,
        grid=(blocks,),
        in_specs=[pl.BlockSpec(gates_bd.shape, lambda i, o, f: (0, 0, 0))]
        + [source_spec(index) for index in range(len(sources))],
        out_specs=out_spec,
        scratch_shapes=[pltpu.VMEM((BLOCK // 2, wide, 2 * lanes), jnp.bfloat16)],
    )
    return pl.pallas_call(
        make_kernel(slab_in, slab_out, len(sources), per_source),
        grid_spec=grid_spec,
        out_shape=jax.ShapeDtypeStruct(out_shape, sources[0].dtype),
        compiler_params=pltpu.CompilerParams(dimension_semantics=("arbitrary",)),
    )(order, flips, gates_bd, *sources)


def swap_major(values):
    amp_count = lax.axis_size("amp")
    wide, slabs, lanes = values.shape
    split = values.reshape(amp_count, wide // amp_count, slabs, lanes)
    swapped = lax.all_to_all(split, "amp", split_axis=0, concat_axis=0, tiled=True)
    return swapped.reshape(wide, slabs, lanes)


def all_sum(values, axes):
    count = lax.axis_size(axes)
    pieces = values.reshape(count, -1).astype(jnp.bfloat16)
    gathered = lax.all_to_all(pieces, axes, split_axis=0, concat_axis=0, tiled=True)
    reduced = jnp.sum(gathered.astype(jnp.float32), axis=0, keepdims=True)
    spread = jnp.broadcast_to(reduced.astype(jnp.bfloat16), pieces.shape)
    whole = lax.all_to_all(spread, axes, split_axis=0, concat_axis=0, tiled=True)
    return whole.reshape(values.shape).astype(jnp.float32)


def on_device(amplitudes, adjoint, gate_mats, gate_order, gate_window, swap_window):
    gates_bd = block_diagonal(gate_mats)
    slabs = amplitudes.shape[0]
    chunk = slabs // CHUNKS
    lanes_window = jnp.int32(0)
    chunks = None
    for segment in range(SEGS):
        order = lax.dynamic_slice_in_dim(gate_order, segment * GATES, GATES)
        window = lax.dynamic_slice_in_dim(gate_window, segment * GATES, GATES)
        before = jnp.concatenate([lanes_window.reshape(1), window[:-1]])
        wanted = 1 - swap_window[segment] if segment < SEGS - 1 else jnp.int32(0)
        flips = jnp.concatenate([window != before, (window[-1] != wanted).reshape(1)])
        flips = flips.astype(jnp.int32)
        lanes_window = wanted
        if segment == 0:
            chunks = [
                run_segment([amplitudes], gates_bd, order, flips, True, False, chunk, c * (chunk // BLOCK))
                for c in range(CHUNKS)
            ]
        elif segment < SEGS - 1:
            chunks = [run_segment([part], gates_bd, order, flips, False, False, chunk) for part in chunks]
        else:
            current = run_segment(chunks, gates_bd, order, flips, False, True, slabs)
        if segment < SEGS - 1:
            chunks = [swap_major(part) for part in chunks]
    order = 4 * amplitudes.shape[2]
    owned_rows = order // lax.axis_size("grp")
    flattened = current.reshape(-1, order)
    adjoint_flat = adjoint.reshape(-1, order)
    partial_correlation = lax.dot_general(
        adjoint_flat, flattened, (((0,), (0,)), ((), ())), preferred_element_type=jnp.float32
    )
    summed = all_sum(partial_correlation, ("amp", "grp"))
    owned = lax.dynamic_slice_in_dim(summed, lax.axis_index("grp") * owned_rows, owned_rows, 0)
    gram = lax.dot_general(
        summed,
        summed,
        (((0,), (0,)), ((), ())),
        precision=lax.Precision.HIGHEST,
        preferred_element_type=jnp.float32,
    )
    scale = 1.0 / jnp.sqrt(jnp.trace(gram) / order + 1e-06)
    product = jnp.dot(owned, gram, precision=lax.Precision.HIGHEST)
    environment = jnp.sqrt(jnp.float32(order)) * (
        1.5 * scale * owned - 0.5 * scale * scale * scale * product
    )
    return (current, environment)


def solution(mesh):
    in_specs = (P(("amp", "grp"), None, None), P(("amp", "grp"), None, None), P(), P(), P(), P())
    out_specs = (P(("amp", "grp"), None, None), P("grp", None))
    return jax.shard_map(
        on_device, mesh=mesh, in_specs=in_specs, out_specs=out_specs, check_vma=False
    )
```

```python
import jax
import jax.numpy as jnp
from jax import lax
from jax.experimental import pallas as pl
from jax.experimental.pallas import tpu as pltpu
from jax.sharding import PartitionSpec as P

SEGS = 4
GATES = 5
BLOCK = 32
CHUNKS = 2


def make_kernel(slab_in, slab_out, sources, blocks_per_source):
    def kernel(order_ref, flip_ref, gates_ref, *refs):
        x_refs, o_ref, held = refs[:sources], refs[sources], refs[sources + 1]
        half, wide, pair = held.shape
        lanes = pair // 2

        def load(x_ref):
            if slab_in:
                slabs = x_ref[...]
            else:
                slabs = jnp.swapaxes(x_ref[...], 0, 1)
            held[:, :, :lanes] = slabs[:half]
            held[:, :, lanes:] = slabs[half:]

        if sources == 1:
            load(x_refs[0])
        else:
            step = pl.program_id(0)
            for index, x_ref in enumerate(x_refs):
                inside = (step >= index * blocks_per_source) & (step < (index + 1) * blocks_per_source)
                pl.when(inside)(lambda x_ref=x_ref: load(x_ref))

        def flip():
            held[:, :, :lanes] = jnp.swapaxes(held[:, :, :lanes], 1, 2)
            held[:, :, lanes:] = jnp.swapaxes(held[:, :, lanes:], 1, 2)

        def one_gate(position):
            matrix = gates_ref[jnp.minimum(order_ref[position], gates_ref.shape[0] - 1)]
            flat = held[...].reshape(half * wide, pair)
            out = jnp.dot(flat, matrix, preferred_element_type=jnp.float32)
            held[...] = out.astype(jnp.bfloat16).reshape(half, wide, pair)

        def one_step(position, carry):
            pl.when(flip_ref[position] == 1)(flip)
            pl.when(position < GATES)(lambda: one_gate(position))
            return carry

        lax.fori_loop(0, GATES + 1, one_step, 0)

        first = held[:, :, :lanes]
        second = held[:, :, lanes:]
        if slab_out:
            o_ref[:half] = first
            o_ref[half:] = second
        else:
            o_ref[:, :half, :] = jnp.swapaxes(first, 0, 1)
            o_ref[:, half:, :] = jnp.swapaxes(second, 0, 1)

    return kernel


def block_diagonal(gate_mats):
    transposed = jnp.swapaxes(gate_mats, 1, 2)
    zeros = jnp.zeros_like(transposed)
    top = jnp.concatenate([transposed, zeros], axis=2)
    bottom = jnp.concatenate([zeros, transposed], axis=2)
    return jnp.concatenate([top, bottom], axis=1)


def run_segment(sources, gates_bd, order, flips, slab_in, slab_out, slabs, offset=0):
    wide = gates_bd.shape[1] // 2
    lanes = sources[0].shape[2]
    blocks = slabs // BLOCK
    per_source = blocks // len(sources)

    def source_spec(index):
        def pick(i, o, f):
            local = jnp.clip(i - index * per_source, 0, per_source - 1) + offset
            return (local, 0, 0) if slab_in else (0, local, 0)

        shape = (BLOCK, wide, lanes) if slab_in else (wide, BLOCK, lanes)
        return pl.BlockSpec(shape, pick)

    if slab_out:
        out_spec = pl.BlockSpec((BLOCK, wide, lanes), lambda i, o, f: (i, 0, 0))
        out_shape = (slabs, wide, lanes)
    else:
        out_spec = pl.BlockSpec((wide, BLOCK, lanes), lambda i, o, f: (0, i, 0))
        out_shape = (wide, slabs, lanes)
    grid_spec = pltpu.PrefetchScalarGridSpec(
        num_scalar_prefetch=2,
        grid=(blocks,),
        in_specs=[pl.BlockSpec(gates_bd.shape, lambda i, o, f: (0, 0, 0))]
        + [source_spec(index) for index in range(len(sources))],
        out_specs=out_spec,
        scratch_shapes=[pltpu.VMEM((BLOCK // 2, wide, 2 * lanes), jnp.bfloat16)],
    )
    return pl.pallas_call(
        make_kernel(slab_in, slab_out, len(sources), per_source),
        grid_spec=grid_spec,
        out_shape=jax.ShapeDtypeStruct(out_shape, sources[0].dtype),
        compiler_params=pltpu.CompilerParams(dimension_semantics=("arbitrary",)),
    )(order, flips, gates_bd, *sources)


def swap_major(values):
    amp_count = lax.axis_size("amp")
    wide, slabs, lanes = values.shape
    split = values.reshape(amp_count, wide // amp_count, slabs, lanes)
    swapped = lax.all_to_all(split, "amp", split_axis=0, concat_axis=0, tiled=True)
    return swapped.reshape(wide, slabs, lanes)


def all_sum(values, axes):
    count = lax.axis_size(axes)
    pieces = values.reshape(count, -1).astype(jnp.bfloat16)
    gathered = lax.all_to_all(pieces, axes, split_axis=0, concat_axis=0, tiled=True)
    reduced = jnp.sum(gathered.astype(jnp.float32), axis=0, keepdims=True)
    spread = jnp.broadcast_to(reduced.astype(jnp.bfloat16), pieces.shape)
    whole = lax.all_to_all(spread, axes, split_axis=0, concat_axis=0, tiled=True)
    return whole.reshape(values.shape).astype(jnp.float32)


def on_device(amplitudes, adjoint, gate_mats, gate_order, gate_window, swap_window):
    gates_bd = block_diagonal(gate_mats)
    slabs = amplitudes.shape[0]
    chunk = slabs // CHUNKS
    lanes_window = jnp.int32(0)
    chunks = None
    for segment in range(SEGS):
        order = lax.dynamic_slice_in_dim(gate_order, segment * GATES, GATES)
        order = jnp.concatenate([order, order[:1]])
        window = lax.dynamic_slice_in_dim(gate_window, segment * GATES, GATES)
        before = jnp.concatenate([lanes_window.reshape(1), window[:-1]])
        wanted = 1 - swap_window[segment] if segment < SEGS - 1 else jnp.int32(0)
        flips = jnp.concatenate([window != before, (window[-1] != wanted).reshape(1)])
        flips = flips.astype(jnp.int32)
        lanes_window = wanted
        if segment == 0:
            chunks = [
                run_segment([amplitudes], gates_bd, order, flips, True, False, chunk, c * (chunk // BLOCK))
                for c in range(CHUNKS)
            ]
        elif segment < SEGS - 1:
            chunks = [run_segment([part], gates_bd, order, flips, False, False, chunk) for part in chunks]
        else:
            finals = [run_segment([part], gates_bd, order, flips, False, True, chunk) for part in chunks]
        if segment < SEGS - 1:
            chunks = [swap_major(part) for part in chunks]
    order = 4 * amplitudes.shape[2]
    owned_rows = order // lax.axis_size("grp")
    adjoint_parts = adjoint.reshape(CHUNKS, chunk * amplitudes.shape[1] // 4, order)
    partial_correlation = sum(
        lax.dot_general(
            adjoint_parts[c], final.reshape(-1, order), (((0,), (0,)), ((), ())),
            preferred_element_type=jnp.float32,
        )
        for c, final in enumerate(finals)
    )
    current = jnp.concatenate(finals, axis=0)
    summed = all_sum(partial_correlation, ("amp", "grp"))
    owned = lax.dynamic_slice_in_dim(summed, lax.axis_index("grp") * owned_rows, owned_rows, 0)
    gram = lax.dot_general(
        summed,
        summed,
        (((0,), (0,)), ((), ())),
        precision=lax.Precision.HIGHEST,
        preferred_element_type=jnp.float32,
    )
    scale = 1.0 / jnp.sqrt(jnp.trace(gram) / order + 1e-06)
    product = jnp.dot(owned, gram, precision=lax.Precision.HIGHEST)
    environment = jnp.sqrt(jnp.float32(order)) * (
        1.5 * scale * owned - 0.5 * scale * scale * scale * product
    )
    return (current, environment)


def solution(mesh):
    in_specs = (P(("amp", "grp"), None, None), P(("amp", "grp"), None, None), P(), P(), P(), P())
    out_specs = (P(("amp", "grp"), None, None), P("grp", None))
    return jax.shard_map(
        on_device, mesh=mesh, in_specs=in_specs, out_specs=out_specs, check_vma=False
    )
```

```python
import jax
import jax.numpy as jnp
from jax import lax
from jax.experimental import pallas as pl
from jax.experimental.pallas import tpu as pltpu
from jax.sharding import PartitionSpec as P

SEGS = 4
GATES = 5
BLOCK = 16
CHUNKS = 2


def make_kernel(slab_in, slab_out, sources, blocks_per_source):
    def kernel(order_ref, flip_ref, gates_ref, *refs):
        x_refs, o_ref, held = refs[:sources], refs[sources], refs[sources + 1]
        half, wide, pair = held.shape
        lanes = pair // 2

        def load(x_ref):
            if slab_in:
                slabs = x_ref[...]
            else:
                slabs = jnp.swapaxes(x_ref[...], 0, 1)
            held[:, :, :lanes] = slabs[:half]
            held[:, :, lanes:] = slabs[half:]

        if sources == 1:
            load(x_refs[0])
        else:
            step = pl.program_id(0)
            for index, x_ref in enumerate(x_refs):
                inside = (step >= index * blocks_per_source) & (step < (index + 1) * blocks_per_source)
                pl.when(inside)(lambda x_ref=x_ref: load(x_ref))

        def flip():
            held[:, :, :lanes] = jnp.swapaxes(held[:, :, :lanes], 1, 2)
            held[:, :, lanes:] = jnp.swapaxes(held[:, :, lanes:], 1, 2)

        def one_gate(position, carry):
            pl.when(flip_ref[position] == 1)(flip)
            matrix = gates_ref[order_ref[position]]
            flat = held[...].reshape(half * wide, pair)
            out = jnp.dot(flat, matrix, preferred_element_type=jnp.float32)
            held[...] = out.astype(jnp.bfloat16).reshape(half, wide, pair)
            return carry

        lax.fori_loop(0, GATES, one_gate, 0)
        pl.when(flip_ref[GATES] == 1)(flip)

        first = held[:, :, :lanes]
        second = held[:, :, lanes:]
        if slab_out:
            o_ref[:half] = first
            o_ref[half:] = second
        else:
            o_ref[:, :half, :] = jnp.swapaxes(first, 0, 1)
            o_ref[:, half:, :] = jnp.swapaxes(second, 0, 1)

    return kernel


def block_diagonal(gate_mats):
    transposed = jnp.swapaxes(gate_mats, 1, 2)
    zeros = jnp.zeros_like(transposed)
    top = jnp.concatenate([transposed, zeros], axis=2)
    bottom = jnp.concatenate([zeros, transposed], axis=2)
    return jnp.concatenate([top, bottom], axis=1)


def run_segment(sources, gates_bd, order, flips, slab_in, slab_out, slabs, offset=0):
    wide = gates_bd.shape[1] // 2
    lanes = sources[0].shape[2]
    blocks = slabs // BLOCK
    per_source = blocks // len(sources)

    def source_spec(index):
        def pick(i, o, f):
            local = jnp.clip(i - index * per_source, 0, per_source - 1) + offset
            return (local, 0, 0) if slab_in else (0, local, 0)

        shape = (BLOCK, wide, lanes) if slab_in else (wide, BLOCK, lanes)
        return pl.BlockSpec(shape, pick)

    if slab_out:
        out_spec = pl.BlockSpec((BLOCK, wide, lanes), lambda i, o, f: (i, 0, 0))
        out_shape = (slabs, wide, lanes)
    else:
        out_spec = pl.BlockSpec((wide, BLOCK, lanes), lambda i, o, f: (0, i, 0))
        out_shape = (wide, slabs, lanes)
    grid_spec = pltpu.PrefetchScalarGridSpec(
        num_scalar_prefetch=2,
        grid=(blocks,),
        in_specs=[pl.BlockSpec(gates_bd.shape, lambda i, o, f: (0, 0, 0))]
        + [source_spec(index) for index in range(len(sources))],
        out_specs=out_spec,
        scratch_shapes=[pltpu.VMEM((BLOCK // 2, wide, 2 * lanes), jnp.bfloat16)],
    )
    return pl.pallas_call(
        make_kernel(slab_in, slab_out, len(sources), per_source),
        grid_spec=grid_spec,
        out_shape=jax.ShapeDtypeStruct(out_shape, sources[0].dtype),
        compiler_params=pltpu.CompilerParams(dimension_semantics=("arbitrary",)),
    )(order, flips, gates_bd, *sources)


def swap_major(values):
    amp_count = lax.axis_size("amp")
    wide, slabs, lanes = values.shape
    split = values.reshape(amp_count, wide // amp_count, slabs, lanes)
    swapped = lax.all_to_all(split, "amp", split_axis=0, concat_axis=0, tiled=True)
    return swapped.reshape(wide, slabs, lanes)


def all_sum(values, axes):
    count = lax.axis_size(axes)
    pieces = values.reshape(count, -1).astype(jnp.bfloat16)
    gathered = lax.all_to_all(pieces, axes, split_axis=0, concat_axis=0, tiled=True)
    reduced = jnp.sum(gathered.astype(jnp.float32), axis=0, keepdims=True)
    spread = jnp.broadcast_to(reduced.astype(jnp.bfloat16), pieces.shape)
    whole = lax.all_to_all(spread, axes, split_axis=0, concat_axis=0, tiled=True)
    return whole.reshape(values.shape).astype(jnp.float32)


def on_device(amplitudes, adjoint, gate_mats, gate_order, gate_window, swap_window):
    gates_bd = block_diagonal(gate_mats)
    slabs = amplitudes.shape[0]
    chunk = slabs // CHUNKS
    lanes_window = jnp.int32(0)
    chunks = None
    for segment in range(SEGS):
        order = lax.dynamic_slice_in_dim(gate_order, segment * GATES, GATES)
        window = lax.dynamic_slice_in_dim(gate_window, segment * GATES, GATES)
        before = jnp.concatenate([lanes_window.reshape(1), window[:-1]])
        wanted = 1 - swap_window[segment] if segment < SEGS - 1 else jnp.int32(0)
        flips = jnp.concatenate([window != before, (window[-1] != wanted).reshape(1)])
        flips = flips.astype(jnp.int32)
        lanes_window = wanted
        if segment == 0:
            chunks = [
                run_segment([amplitudes], gates_bd, order, flips, True, False, chunk, c * (chunk // BLOCK))
                for c in range(CHUNKS)
            ]
        elif segment < SEGS - 1:
            chunks = [run_segment([part], gates_bd, order, flips, False, False, chunk) for part in chunks]
        else:
            current = run_segment(chunks, gates_bd, order, flips, False, True, slabs)
        if segment < SEGS - 1:
            chunks = [swap_major(part) for part in chunks]
    order = 4 * amplitudes.shape[2]
    owned_rows = order // lax.axis_size("grp")
    flattened = current.reshape(-1, order)
    adjoint_flat = adjoint.reshape(-1, order)
    partial_correlation = lax.dot_general(
        adjoint_flat, flattened, (((0,), (0,)), ((), ())), preferred_element_type=jnp.float32
    )
    summed = all_sum(partial_correlation, ("amp", "grp"))
    owned = lax.dynamic_slice_in_dim(summed, lax.axis_index("grp") * owned_rows, owned_rows, 0)
    gram = lax.dot_general(
        summed,
        summed,
        (((0,), (0,)), ((), ())),
        precision=lax.Precision.HIGHEST,
        preferred_element_type=jnp.float32,
    )
    scale = 1.0 / jnp.sqrt(jnp.trace(gram) / order + 1e-06)
    product = jnp.dot(owned, gram, precision=lax.Precision.HIGHEST)
    environment = jnp.sqrt(jnp.float32(order)) * (
        1.5 * scale * owned - 0.5 * scale * scale * scale * product
    )
    return (current, environment)


def solution(mesh):
    in_specs = (P(("amp", "grp"), None, None), P(("amp", "grp"), None, None), P(), P(), P(), P())
    out_specs = (P(("amp", "grp"), None, None), P("grp", None))
    return jax.shard_map(
        on_device, mesh=mesh, in_specs=in_specs, out_specs=out_specs, check_vma=False
    )
```

```python
import jax
import jax.numpy as jnp
from jax import lax
from jax.experimental import pallas as pl
from jax.experimental.pallas import tpu as pltpu
from jax.sharding import PartitionSpec as P

SEGS = 4
GATES = 5
BLOCK = 16
CHUNKS = 2


def make_kernel(slab_in, slab_out, sources, blocks_per_source, segment):
    def kernel(order_ref, flip_ref, gates_ref, *refs):
        x_refs, o_ref, held = refs[:sources], refs[sources], refs[sources + 1]
        half, wide, pair = held.shape
        lanes = pair // 2

        def load(x_ref):
            if slab_in:
                slabs = x_ref[...]
            else:
                slabs = jnp.swapaxes(x_ref[...], 0, 1)
            held[:, :, :lanes] = slabs[:half]
            held[:, :, lanes:] = slabs[half:]

        if sources == 1:
            load(x_refs[0])
        else:
            step = pl.program_id(0)
            for index, x_ref in enumerate(x_refs):
                inside = (step >= index * blocks_per_source) & (step < (index + 1) * blocks_per_source)
                pl.when(inside)(lambda x_ref=x_ref: load(x_ref))

        def flip():
            held[:, :, :lanes] = jnp.swapaxes(held[:, :, :lanes], 1, 2)
            held[:, :, lanes:] = jnp.swapaxes(held[:, :, lanes:], 1, 2)

        def one_gate(position, carry):
            pl.when(flip_ref[segment, position] == 1)(flip)
            matrix = gates_ref[order_ref[segment, position]]
            flat = held[...].reshape(half * wide, pair)
            out = lax.dot_general(
                flat, matrix, (((1,), (1,)), ((), ())), preferred_element_type=jnp.float32
            )
            held[...] = out.astype(jnp.bfloat16).reshape(half, wide, pair)
            return carry

        lax.fori_loop(0, GATES, one_gate, 0)
        pl.when(flip_ref[segment, GATES] == 1)(flip)

        first = held[:, :, :lanes]
        second = held[:, :, lanes:]
        if slab_out:
            o_ref[:half] = first
            o_ref[half:] = second
        else:
            o_ref[:, :half, :] = jnp.swapaxes(first, 0, 1)
            o_ref[:, half:, :] = jnp.swapaxes(second, 0, 1)

    return kernel


def block_diagonal(gate_mats):
    zeros = jnp.zeros_like(gate_mats)
    top = jnp.concatenate([gate_mats, zeros], axis=2)
    bottom = jnp.concatenate([zeros, gate_mats], axis=2)
    return jnp.concatenate([top, bottom], axis=1)


def run_segment(sources, gates_bd, order, flips, segment, slab_in, slab_out, slabs, offset=0):
    wide = gates_bd.shape[1] // 2
    lanes = sources[0].shape[2]
    blocks = slabs // BLOCK
    per_source = blocks // len(sources)

    def source_spec(index):
        def pick(i, o, f):
            local = jnp.clip(i - index * per_source, 0, per_source - 1) + offset
            return (local, 0, 0) if slab_in else (0, local, 0)

        shape = (BLOCK, wide, lanes) if slab_in else (wide, BLOCK, lanes)
        return pl.BlockSpec(shape, pick)

    if slab_out:
        out_spec = pl.BlockSpec((BLOCK, wide, lanes), lambda i, o, f: (i, 0, 0))
        out_shape = (slabs, wide, lanes)
    else:
        out_spec = pl.BlockSpec((wide, BLOCK, lanes), lambda i, o, f: (0, i, 0))
        out_shape = (wide, slabs, lanes)
    grid_spec = pltpu.PrefetchScalarGridSpec(
        num_scalar_prefetch=2,
        grid=(blocks,),
        in_specs=[pl.BlockSpec(gates_bd.shape, lambda i, o, f: (0, 0, 0))]
        + [source_spec(index) for index in range(len(sources))],
        out_specs=out_spec,
        scratch_shapes=[pltpu.VMEM((BLOCK // 2, wide, 2 * lanes), jnp.bfloat16)],
    )
    return pl.pallas_call(
        make_kernel(slab_in, slab_out, len(sources), per_source, segment),
        grid_spec=grid_spec,
        out_shape=jax.ShapeDtypeStruct(out_shape, sources[0].dtype),
        compiler_params=pltpu.CompilerParams(dimension_semantics=("arbitrary",)),
    )(order, flips, gates_bd, *sources)


def swap_major(values):
    amp_count = lax.axis_size("amp")
    wide, slabs, lanes = values.shape
    split = values.reshape(amp_count, wide // amp_count, slabs, lanes)
    swapped = lax.all_to_all(split, "amp", split_axis=0, concat_axis=0, tiled=True)
    return swapped.reshape(wide, slabs, lanes)


def all_sum(values, axes):
    count = lax.axis_size(axes)
    pieces = values.reshape(count, -1, 128).astype(jnp.bfloat16)
    gathered = lax.all_to_all(pieces, axes, split_axis=0, concat_axis=0, tiled=True)
    reduced = jnp.sum(gathered.astype(jnp.float32), axis=0, keepdims=True)
    spread = jnp.broadcast_to(reduced.astype(jnp.bfloat16), pieces.shape)
    whole = lax.all_to_all(spread, axes, split_axis=0, concat_axis=0, tiled=True)
    return whole.reshape(values.shape).astype(jnp.float32)


def on_device(amplitudes, adjoint, gate_mats, gate_order, gate_window, swap_window):
    gates_bd = block_diagonal(gate_mats)
    slabs = amplitudes.shape[0]
    chunk = slabs // CHUNKS
    windows = gate_window.reshape(SEGS, GATES)
    starting = jnp.concatenate([jnp.zeros((1,), jnp.int32), 1 - swap_window])
    wanted = jnp.concatenate([1 - swap_window, jnp.zeros((1,), jnp.int32)])
    before = jnp.concatenate([starting[:, None], windows[:, :-1]], axis=1)
    flips = jnp.concatenate([windows != before, (windows[:, -1] != wanted)[:, None]], axis=1)
    flips = flips.astype(jnp.int32)
    order = gate_order.reshape(SEGS, GATES)
    chunks = None
    for segment in range(SEGS):
        if segment == 0:
            chunks = [
                run_segment([amplitudes], gates_bd, order, flips, segment, True, False, chunk, c * (chunk // BLOCK))
                for c in range(CHUNKS)
            ]
        elif segment < SEGS - 1:
            chunks = [run_segment([part], gates_bd, order, flips, segment, False, False, chunk) for part in chunks]
        else:
            current = run_segment(chunks, gates_bd, order, flips, segment, False, True, slabs)
        if segment < SEGS - 1:
            chunks = [swap_major(part) for part in chunks]
    order = 4 * amplitudes.shape[2]
    owned_rows = order // lax.axis_size("grp")
    flattened = current.reshape(-1, order)
    adjoint_flat = adjoint.reshape(-1, order)
    partial_correlation = lax.dot_general(
        adjoint_flat, flattened, (((0,), (0,)), ((), ())), preferred_element_type=jnp.float32
    )
    summed = all_sum(partial_correlation, ("amp", "grp"))
    owned = lax.dynamic_slice_in_dim(summed, lax.axis_index("grp") * owned_rows, owned_rows, 0)
    gram = lax.dot_general(
        summed,
        summed,
        (((0,), (0,)), ((), ())),
        precision=lax.Precision.HIGHEST,
        preferred_element_type=jnp.float32,
    )
    scale = 1.0 / jnp.sqrt(jnp.trace(gram) / order + 1e-06)
    product = jnp.dot(owned, gram, precision=lax.Precision.HIGHEST)
    environment = jnp.sqrt(jnp.float32(order)) * (
        1.5 * scale * owned - 0.5 * scale * scale * scale * product
    )
    return (current, environment)


def solution(mesh):
    in_specs = (P(("amp", "grp"), None, None), P(("amp", "grp"), None, None), P(), P(), P(), P())
    out_specs = (P(("amp", "grp"), None, None), P("grp", None))
    return jax.shard_map(
        on_device, mesh=mesh, in_specs=in_specs, out_specs=out_specs, check_vma=False
    )
```

```python
import jax
import jax.numpy as jnp
from jax import lax
from jax.experimental import pallas as pl
from jax.experimental.pallas import tpu as pltpu
from jax.sharding import PartitionSpec as P

SEGS = 4
GATES = 5
BLOCK = 16
CHUNKS = 2


def make_kernel(slab_in, slab_out, sources, blocks_per_source, segment):
    def kernel(order_ref, flip_ref, gates_ref, *refs):
        x_refs, o_ref, held = refs[:sources], refs[-2], refs[-1]
        half, wide, pair = held.shape
        lanes = pair // 2

        def load(x_ref):
            if slab_in:
                slabs = x_ref[...]
            else:
                slabs = jnp.swapaxes(x_ref[...], 0, 1)
            held[:, :, :lanes] = slabs[:half]
            held[:, :, lanes:] = slabs[half:]

        if sources == 1:
            load(x_refs[0])
        else:
            step = pl.program_id(0)
            for index, x_ref in enumerate(x_refs):
                inside = (step >= index * blocks_per_source) & (step < (index + 1) * blocks_per_source)
                pl.when(inside)(lambda x_ref=x_ref: load(x_ref))

        def flip():
            held[:, :, :lanes] = jnp.swapaxes(held[:, :, :lanes], 1, 2)
            held[:, :, lanes:] = jnp.swapaxes(held[:, :, lanes:], 1, 2)

        def one_gate(position, carry):
            pl.when(flip_ref[segment, position] == 1)(flip)
            matrix = gates_ref[order_ref[segment, position]]
            flat = held[...].reshape(half * wide, pair)
            out = lax.dot_general(
                flat, matrix, (((1,), (1,)), ((), ())), preferred_element_type=jnp.float32
            )
            held[...] = out.astype(jnp.bfloat16).reshape(half, wide, pair)
            return carry

        lax.fori_loop(0, GATES, one_gate, 0)
        pl.when(flip_ref[segment, GATES] == 1)(flip)

        first = held[:, :, :lanes]
        second = held[:, :, lanes:]
        if slab_out:
            o_ref[:half] = first
            o_ref[half:] = second
        else:
            o_ref[:, :half, :] = jnp.swapaxes(first, 0, 1)
            o_ref[:, half:, :] = jnp.swapaxes(second, 0, 1)

    return kernel


def block_diagonal(gate_mats):
    zeros = jnp.zeros_like(gate_mats)
    top = jnp.concatenate([gate_mats, zeros], axis=2)
    bottom = jnp.concatenate([zeros, gate_mats], axis=2)
    return jnp.concatenate([top, bottom], axis=1)


def run_segment(sources, gates_bd, order, flips, segment, slab_in, slab_out, slabs, offset=0,
                into=None, out_offset=0, out_slabs=None):
    wide = gates_bd.shape[1] // 2
    lanes = sources[0].shape[2]
    blocks = slabs // BLOCK
    per_source = blocks // len(sources)

    def source_spec(index):
        def pick(i, o, f):
            local = jnp.clip(i - index * per_source, 0, per_source - 1) + offset
            return (local, 0, 0) if slab_in else (0, local, 0)

        shape = (BLOCK, wide, lanes) if slab_in else (wide, BLOCK, lanes)
        return pl.BlockSpec(shape, pick)

    if slab_out:
        out_spec = pl.BlockSpec((BLOCK, wide, lanes), lambda i, o, f: (i + out_offset, 0, 0))
        out_shape = (out_slabs or slabs, wide, lanes)
    else:
        out_spec = pl.BlockSpec((wide, BLOCK, lanes), lambda i, o, f: (0, i, 0))
        out_shape = (wide, slabs, lanes)
    grid_spec = pltpu.PrefetchScalarGridSpec(
        num_scalar_prefetch=2,
        grid=(blocks,),
        in_specs=[pl.BlockSpec(gates_bd.shape, lambda i, o, f: (0, 0, 0))]
        + [source_spec(index) for index in range(len(sources))]
        + ([] if into is None else [pl.BlockSpec(memory_space=pl.ANY)]),
        out_specs=out_spec,
        scratch_shapes=[pltpu.VMEM((BLOCK // 2, wide, 2 * lanes), jnp.bfloat16)],
    )
    return pl.pallas_call(
        make_kernel(slab_in, slab_out, len(sources), per_source, segment),
        grid_spec=grid_spec,
        out_shape=jax.ShapeDtypeStruct(out_shape, sources[0].dtype),
        compiler_params=pltpu.CompilerParams(dimension_semantics=("arbitrary",)),
        input_output_aliases={} if into is None else {3 + len(sources): 0},
    )(order, flips, gates_bd, *sources, *([] if into is None else [into]))


def swap_major(values):
    amp_count = lax.axis_size("amp")
    wide, slabs, lanes = values.shape
    split = values.reshape(amp_count, wide // amp_count, slabs, lanes)
    swapped = lax.all_to_all(split, "amp", split_axis=0, concat_axis=0, tiled=True)
    return swapped.reshape(wide, slabs, lanes)


def all_sum(values, axes):
    count = lax.axis_size(axes)
    pieces = values.reshape(count, -1, 128).astype(jnp.bfloat16)
    gathered = lax.all_to_all(pieces, axes, split_axis=0, concat_axis=0, tiled=True)
    reduced = jnp.sum(gathered.astype(jnp.float32), axis=0, keepdims=True)
    spread = jnp.broadcast_to(reduced.astype(jnp.bfloat16), pieces.shape)
    whole = lax.all_to_all(spread, axes, split_axis=0, concat_axis=0, tiled=True)
    return whole.reshape(values.shape).astype(jnp.float32)


def on_device(amplitudes, adjoint, gate_mats, gate_order, gate_window, swap_window):
    gates_bd = block_diagonal(gate_mats)
    slabs = amplitudes.shape[0]
    chunk = slabs // CHUNKS
    windows = gate_window.reshape(SEGS, GATES)
    starting = jnp.concatenate([jnp.zeros((1,), jnp.int32), 1 - swap_window])
    wanted = jnp.concatenate([1 - swap_window, jnp.zeros((1,), jnp.int32)])
    before = jnp.concatenate([starting[:, None], windows[:, :-1]], axis=1)
    flips = jnp.concatenate([windows != before, (windows[:, -1] != wanted)[:, None]], axis=1)
    flips = flips.astype(jnp.int32)
    order = gate_order.reshape(SEGS, GATES)
    chunks = None
    for segment in range(SEGS):
        if segment == 0:
            chunks = [
                run_segment([amplitudes], gates_bd, order, flips, segment, True, False, chunk, c * (chunk // BLOCK))
                for c in range(CHUNKS)
            ]
        elif segment < SEGS - 1:
            chunks = [run_segment([part], gates_bd, order, flips, segment, False, False, chunk) for part in chunks]
        else:
            current = None
            for c, part in enumerate(chunks):
                current = run_segment(
                    [part], gates_bd, order, flips, segment, False, True, chunk,
                    into=current, out_offset=c * (chunk // BLOCK), out_slabs=slabs,
                )
        if segment < SEGS - 1:
            chunks = [swap_major(part) for part in chunks]
    order = 4 * amplitudes.shape[2]
    owned_rows = order // lax.axis_size("grp")
    flattened = current.reshape(-1, order)
    adjoint_flat = adjoint.reshape(-1, order)
    partial_correlation = lax.dot_general(
        adjoint_flat, flattened, (((0,), (0,)), ((), ())), preferred_element_type=jnp.float32
    )
    summed = all_sum(partial_correlation, ("amp", "grp"))
    owned = lax.dynamic_slice_in_dim(summed, lax.axis_index("grp") * owned_rows, owned_rows, 0)
    gram = lax.dot_general(
        summed,
        summed,
        (((0,), (0,)), ((), ())),
        precision=lax.Precision.HIGHEST,
        preferred_element_type=jnp.float32,
    )
    scale = 1.0 / jnp.sqrt(jnp.trace(gram) / order + 1e-06)
    product = jnp.dot(owned, gram, precision=lax.Precision.HIGHEST)
    environment = jnp.sqrt(jnp.float32(order)) * (
        1.5 * scale * owned - 0.5 * scale * scale * scale * product
    )
    return (current, environment)


def solution(mesh):
    in_specs = (P(("amp", "grp"), None, None), P(("amp", "grp"), None, None), P(), P(), P(), P())
    out_specs = (P(("amp", "grp"), None, None), P("grp", None))
    return jax.shard_map(
        on_device, mesh=mesh, in_specs=in_specs, out_specs=out_specs, check_vma=False
    )
```

```python
import jax
import jax.numpy as jnp
from jax import lax
from jax.experimental import pallas as pl
from jax.experimental.pallas import tpu as pltpu
from jax.sharding import PartitionSpec as P

SEGS = 4
GATES = 5
BLOCK = 16
CHUNKS = 2


def make_kernel(slab_in, slab_out, sources, blocks_per_source, segment):
    def kernel(order_ref, flip_ref, gates_ref, *refs):
        x_refs, o_ref, held = refs[:sources], refs[-2], refs[-1]
        half, wide, pair = held.shape
        lanes = pair // 2

        def load(x_ref):
            if slab_in:
                slabs = x_ref[...]
            else:
                slabs = jnp.swapaxes(x_ref[...], 0, 1)
            held[:, :, :lanes] = slabs[:half]
            held[:, :, lanes:] = slabs[half:]

        if sources == 1:
            load(x_refs[0])
        else:
            step = pl.program_id(0)
            for index, x_ref in enumerate(x_refs):
                inside = (step >= index * blocks_per_source) & (step < (index + 1) * blocks_per_source)
                pl.when(inside)(lambda x_ref=x_ref: load(x_ref))

        def flip():
            held[:, :, :lanes] = jnp.swapaxes(held[:, :, :lanes], 1, 2)
            held[:, :, lanes:] = jnp.swapaxes(held[:, :, lanes:], 1, 2)

        def one_gate(position, carry):
            pl.when(flip_ref[segment, position] == 1)(flip)
            matrix = gates_ref[order_ref[segment, position]]
            flat = held[...].reshape(half * wide, pair)
            out = lax.dot_general(
                flat, matrix, (((1,), (1,)), ((), ())), preferred_element_type=jnp.float32
            )
            held[...] = out.astype(jnp.bfloat16).reshape(half, wide, pair)
            return carry

        lax.fori_loop(0, GATES, one_gate, 0)
        pl.when(flip_ref[segment, GATES] == 1)(flip)

        first = held[:, :, :lanes]
        second = held[:, :, lanes:]
        if slab_out:
            o_ref[:half] = first
            o_ref[half:] = second
        else:
            o_ref[:, :half, :] = jnp.swapaxes(first, 0, 1)
            o_ref[:, half:, :] = jnp.swapaxes(second, 0, 1)

    return kernel


def block_diagonal(gate_mats):
    zeros = jnp.zeros_like(gate_mats)
    top = jnp.concatenate([gate_mats, zeros], axis=2)
    bottom = jnp.concatenate([zeros, gate_mats], axis=2)
    return jnp.concatenate([top, bottom], axis=1)


def run_segment(sources, gates_bd, order, flips, segment, slab_in, slab_out, slabs, offset=0,
                into=None, out_offset=0, out_slabs=None):
    wide = gates_bd.shape[1] // 2
    lanes = sources[0].shape[2]
    blocks = slabs // BLOCK
    per_source = blocks // len(sources)

    def source_spec(index):
        def pick(i, o, f):
            local = jnp.clip(i - index * per_source, 0, per_source - 1) + offset
            return (local, 0, 0) if slab_in else (0, local, 0)

        shape = (BLOCK, wide, lanes) if slab_in else (wide, BLOCK, lanes)
        return pl.BlockSpec(shape, pick)

    if slab_out:
        out_spec = pl.BlockSpec((BLOCK, wide, lanes), lambda i, o, f: (i + out_offset, 0, 0))
        out_shape = (out_slabs or slabs, wide, lanes)
    else:
        out_spec = pl.BlockSpec((wide, BLOCK, lanes), lambda i, o, f: (0, i, 0))
        out_shape = (wide, slabs, lanes)
    grid_spec = pltpu.PrefetchScalarGridSpec(
        num_scalar_prefetch=2,
        grid=(blocks,),
        in_specs=[pl.BlockSpec(gates_bd.shape, lambda i, o, f: (0, 0, 0))]
        + [source_spec(index) for index in range(len(sources))]
        + ([] if into is None else [pl.BlockSpec(memory_space=pl.ANY)]),
        out_specs=out_spec,
        scratch_shapes=[pltpu.VMEM((BLOCK // 2, wide, 2 * lanes), jnp.bfloat16)],
    )
    return pl.pallas_call(
        make_kernel(slab_in, slab_out, len(sources), per_source, segment),
        grid_spec=grid_spec,
        out_shape=jax.ShapeDtypeStruct(out_shape, sources[0].dtype),
        compiler_params=pltpu.CompilerParams(dimension_semantics=("arbitrary",)),
        input_output_aliases={} if into is None else {3 + len(sources): 0},
    )(order, flips, gates_bd, *sources, *([] if into is None else [into]))


def swap_major(values):
    amp_count = lax.axis_size("amp")
    wide, slabs, lanes = values.shape
    split = values.reshape(amp_count, wide // amp_count, slabs, lanes)
    swapped = lax.all_to_all(split, "amp", split_axis=0, concat_axis=0, tiled=True)
    return swapped.reshape(wide, slabs, lanes)


def all_sum(values, axes):
    count = lax.axis_size(axes)
    pieces = values.reshape(count, -1, 128).astype(jnp.bfloat16)
    gathered = lax.all_to_all(pieces, axes, split_axis=0, concat_axis=0, tiled=True)
    reduced = jnp.sum(gathered.astype(jnp.float32), axis=0, keepdims=True)
    spread = jnp.broadcast_to(reduced.astype(jnp.bfloat16), pieces.shape)
    whole = lax.all_to_all(spread, axes, split_axis=0, concat_axis=0, tiled=True)
    return whole.reshape(values.shape).astype(jnp.float32)


def on_device(amplitudes, adjoint, gate_mats, gate_order, gate_window, swap_window):
    gates_bd = block_diagonal(gate_mats)
    slabs = amplitudes.shape[0]
    chunk = slabs // CHUNKS
    windows = gate_window.reshape(SEGS, GATES)
    starting = jnp.concatenate([jnp.zeros((1,), jnp.int32), 1 - swap_window])
    wanted = jnp.concatenate([1 - swap_window, jnp.zeros((1,), jnp.int32)])
    before = jnp.concatenate([starting[:, None], windows[:, :-1]], axis=1)
    flips = jnp.concatenate([windows != before, (windows[:, -1] != wanted)[:, None]], axis=1)
    flips = flips.astype(jnp.int32)
    order = gate_order.reshape(SEGS, GATES)
    chunks = None
    for segment in range(SEGS):
        if segment == 0:
            chunks = [
                run_segment([amplitudes], gates_bd, order, flips, segment, True, False, chunk, c * (chunk // BLOCK))
                for c in range(CHUNKS)
            ]
        elif segment < SEGS - 1:
            chunks = [run_segment([part], gates_bd, order, flips, segment, False, False, chunk) for part in chunks]
        else:
            finals = [run_segment([part], gates_bd, order, flips, segment, False, True, chunk) for part in chunks]
        if segment < SEGS - 1:
            chunks = [swap_major(part) for part in chunks]
    order = 4 * amplitudes.shape[2]
    owned_rows = order // lax.axis_size("grp")
    adjoint_flat = adjoint.reshape(-1, order)
    rows = adjoint_flat.shape[0] // CHUNKS
    partial_correlation = sum(
        lax.dot_general(
            adjoint_flat[c * rows:(c + 1) * rows], final.reshape(-1, order), (((0,), (0,)), ((), ())),
            preferred_element_type=jnp.float32,
        )
        for c, final in enumerate(finals)
    )
    current = jnp.concatenate(finals, axis=0)
    summed = all_sum(partial_correlation, ("amp", "grp"))
    owned = lax.dynamic_slice_in_dim(summed, lax.axis_index("grp") * owned_rows, owned_rows, 0)
    gram = lax.dot_general(
        summed,
        summed,
        (((0,), (0,)), ((), ())),
        precision=lax.Precision.HIGHEST,
        preferred_element_type=jnp.float32,
    )
    scale = 1.0 / jnp.sqrt(jnp.trace(gram) / order + 1e-06)
    product = jnp.dot(owned, gram, precision=lax.Precision.HIGHEST)
    environment = jnp.sqrt(jnp.float32(order)) * (
        1.5 * scale * owned - 0.5 * scale * scale * scale * product
    )
    return (current, environment)


def solution(mesh):
    in_specs = (P(("amp", "grp"), None, None), P(("amp", "grp"), None, None), P(), P(), P(), P())
    out_specs = (P(("amp", "grp"), None, None), P("grp", None))
    return jax.shard_map(
        on_device, mesh=mesh, in_specs=in_specs, out_specs=out_specs, check_vma=False
    )
```

```python
import jax
import jax.numpy as jnp
from jax import lax
from jax.experimental import pallas as pl
from jax.experimental.pallas import tpu as pltpu
from jax.sharding import PartitionSpec as P

SEGS = 4
GATES = 5
BLOCK = 16
CHUNKS = 2


def make_kernel(slab_in, slab_out, sources, blocks_per_source, segment):
    def kernel(order_ref, flip_ref, gates_ref, *refs):
        x_refs, o_ref, held, diagonal = refs[:sources], refs[-3], refs[-2], refs[-1]
        half, wide, pair = held.shape
        lanes = pair // 2

        @pl.when(pl.program_id(0) == 0)
        def _():
            diagonal[...] = jnp.zeros(diagonal.shape, diagonal.dtype)
            for position in range(GATES):
                matrix = gates_ref[order_ref[segment, position]]
                diagonal[position, :lanes, :lanes] = matrix
                diagonal[position, lanes:, lanes:] = matrix

        def load(x_ref):
            if slab_in:
                slabs = x_ref[...]
            else:
                slabs = jnp.swapaxes(x_ref[...], 0, 1)
            held[:, :, :lanes] = slabs[:half]
            held[:, :, lanes:] = slabs[half:]

        if sources == 1:
            load(x_refs[0])
        else:
            step = pl.program_id(0)
            for index, x_ref in enumerate(x_refs):
                inside = (step >= index * blocks_per_source) & (step < (index + 1) * blocks_per_source)
                pl.when(inside)(lambda x_ref=x_ref: load(x_ref))

        def flip():
            held[:, :, :lanes] = jnp.swapaxes(held[:, :, :lanes], 1, 2)
            held[:, :, lanes:] = jnp.swapaxes(held[:, :, lanes:], 1, 2)

        def one_gate(position, carry):
            pl.when(flip_ref[segment, position] == 1)(flip)
            matrix = diagonal[position]
            flat = held[...].reshape(half * wide, pair)
            out = lax.dot_general(
                flat, matrix, (((1,), (1,)), ((), ())), preferred_element_type=jnp.float32
            )
            held[...] = out.astype(jnp.bfloat16).reshape(half, wide, pair)
            return carry

        lax.fori_loop(0, GATES, one_gate, 0)
        pl.when(flip_ref[segment, GATES] == 1)(flip)

        first = held[:, :, :lanes]
        second = held[:, :, lanes:]
        if slab_out:
            o_ref[:half] = first
            o_ref[half:] = second
        else:
            o_ref[:, :half, :] = jnp.swapaxes(first, 0, 1)
            o_ref[:, half:, :] = jnp.swapaxes(second, 0, 1)

    return kernel


def run_segment(sources, gate_mats, order, flips, segment, slab_in, slab_out, slabs, offset=0,
                into=None, out_offset=0, out_slabs=None):
    wide = gate_mats.shape[1]
    lanes = sources[0].shape[2]
    blocks = slabs // BLOCK
    per_source = blocks // len(sources)

    def source_spec(index):
        def pick(i, o, f):
            local = jnp.clip(i - index * per_source, 0, per_source - 1) + offset
            return (local, 0, 0) if slab_in else (0, local, 0)

        shape = (BLOCK, wide, lanes) if slab_in else (wide, BLOCK, lanes)
        return pl.BlockSpec(shape, pick)

    if slab_out:
        out_spec = pl.BlockSpec((BLOCK, wide, lanes), lambda i, o, f: (i + out_offset, 0, 0))
        out_shape = (out_slabs or slabs, wide, lanes)
    else:
        out_spec = pl.BlockSpec((wide, BLOCK, lanes), lambda i, o, f: (0, i, 0))
        out_shape = (wide, slabs, lanes)
    grid_spec = pltpu.PrefetchScalarGridSpec(
        num_scalar_prefetch=2,
        grid=(blocks,),
        in_specs=[pl.BlockSpec(gate_mats.shape, lambda i, o, f: (0, 0, 0))]
        + [source_spec(index) for index in range(len(sources))]
        + ([] if into is None else [pl.BlockSpec(memory_space=pl.ANY)]),
        out_specs=out_spec,
        scratch_shapes=[
            pltpu.VMEM((BLOCK // 2, wide, 2 * lanes), jnp.bfloat16),
            pltpu.VMEM((GATES, 2 * wide, 2 * lanes), jnp.bfloat16),
        ],
    )
    return pl.pallas_call(
        make_kernel(slab_in, slab_out, len(sources), per_source, segment),
        grid_spec=grid_spec,
        out_shape=jax.ShapeDtypeStruct(out_shape, sources[0].dtype),
        compiler_params=pltpu.CompilerParams(dimension_semantics=("arbitrary",)),
        input_output_aliases={} if into is None else {3 + len(sources): 0},
    )(order, flips, gate_mats, *sources, *([] if into is None else [into]))


def swap_major(values):
    amp_count = lax.axis_size("amp")
    wide, slabs, lanes = values.shape
    split = values.reshape(amp_count, wide // amp_count, slabs, lanes)
    swapped = lax.all_to_all(split, "amp", split_axis=0, concat_axis=0, tiled=True)
    return swapped.reshape(wide, slabs, lanes)


def all_sum(values, axes):
    count = lax.axis_size(axes)
    pieces = values.reshape(count, -1, 128).astype(jnp.bfloat16)
    gathered = lax.all_to_all(pieces, axes, split_axis=0, concat_axis=0, tiled=True)
    reduced = jnp.sum(gathered.astype(jnp.float32), axis=0, keepdims=True)
    spread = jnp.broadcast_to(reduced.astype(jnp.bfloat16), pieces.shape)
    whole = lax.all_to_all(spread, axes, split_axis=0, concat_axis=0, tiled=True)
    return whole.reshape(values.shape).astype(jnp.float32)


def on_device(amplitudes, adjoint, gate_mats, gate_order, gate_window, swap_window):
    slabs = amplitudes.shape[0]
    chunk = slabs // CHUNKS
    windows = gate_window.reshape(SEGS, GATES)
    starting = jnp.concatenate([jnp.zeros((1,), jnp.int32), 1 - swap_window])
    wanted = jnp.concatenate([1 - swap_window, jnp.zeros((1,), jnp.int32)])
    before = jnp.concatenate([starting[:, None], windows[:, :-1]], axis=1)
    flips = jnp.concatenate([windows != before, (windows[:, -1] != wanted)[:, None]], axis=1)
    flips = flips.astype(jnp.int32)
    order = gate_order.reshape(SEGS, GATES)
    chunks = None
    for segment in range(SEGS):
        if segment == 0:
            chunks = [
                run_segment([amplitudes], gate_mats, order, flips, segment, True, False, chunk, c * (chunk // BLOCK))
                for c in range(CHUNKS)
            ]
        elif segment < SEGS - 1:
            chunks = [run_segment([part], gate_mats, order, flips, segment, False, False, chunk) for part in chunks]
        else:
            finals = [run_segment([part], gate_mats, order, flips, segment, False, True, chunk) for part in chunks]
        if segment < SEGS - 1:
            chunks = [swap_major(part) for part in chunks]
    order = 4 * amplitudes.shape[2]
    owned_rows = order // lax.axis_size("grp")
    adjoint_flat = adjoint.reshape(-1, order)
    rows = adjoint_flat.shape[0] // CHUNKS
    partial_correlation = sum(
        lax.dot_general(
            adjoint_flat[c * rows:(c + 1) * rows], final.reshape(-1, order), (((0,), (0,)), ((), ())),
            preferred_element_type=jnp.float32,
        )
        for c, final in enumerate(finals)
    )
    current = jnp.concatenate(finals, axis=0)
    summed = all_sum(partial_correlation, ("amp", "grp"))
    owned = lax.dynamic_slice_in_dim(summed, lax.axis_index("grp") * owned_rows, owned_rows, 0)
    gram = lax.dot_general(
        summed,
        summed,
        (((0,), (0,)), ((), ())),
        precision=lax.Precision.HIGHEST,
        preferred_element_type=jnp.float32,
    )
    scale = 1.0 / jnp.sqrt(jnp.trace(gram) / order + 1e-06)
    product = jnp.dot(owned, gram, precision=lax.Precision.HIGHEST)
    environment = jnp.sqrt(jnp.float32(order)) * (
        1.5 * scale * owned - 0.5 * scale * scale * scale * product
    )
    return (current, environment)


def solution(mesh):
    in_specs = (P(("amp", "grp"), None, None), P(("amp", "grp"), None, None), P(), P(), P(), P())
    out_specs = (P(("amp", "grp"), None, None), P("grp", None))
    return jax.shard_map(
        on_device, mesh=mesh, in_specs=in_specs, out_specs=out_specs, check_vma=False
    )
```

```python
import jax
import jax.numpy as jnp
from jax import lax
from jax.experimental import pallas as pl
from jax.experimental.pallas import tpu as pltpu
from jax.sharding import PartitionSpec as P

SEGS = 4
GATES = 5
BLOCK = 32
CHUNKS = 2


def make_kernel(slab_in, slab_out, sources, blocks_per_source, segment):
    def kernel(order_ref, flip_ref, gates_ref, *refs):
        x_refs, o_ref, held, diagonal = refs[:sources], refs[-3], refs[-2], refs[-1]
        half, wide, pair = held.shape
        lanes = pair // 2

        @pl.when(pl.program_id(0) == 0)
        def _():
            diagonal[...] = jnp.zeros(diagonal.shape, diagonal.dtype)
            for position in range(GATES):
                matrix = gates_ref[order_ref[segment, position]]
                diagonal[position, :lanes, :lanes] = matrix
                diagonal[position, lanes:, lanes:] = matrix

        def load(x_ref):
            if slab_in:
                slabs = x_ref[...]
            else:
                slabs = jnp.swapaxes(x_ref[...], 0, 1)
            held[:, :, :lanes] = slabs[:half]
            held[:, :, lanes:] = slabs[half:]

        if sources == 1:
            load(x_refs[0])
        else:
            step = pl.program_id(0)
            for index, x_ref in enumerate(x_refs):
                inside = (step >= index * blocks_per_source) & (step < (index + 1) * blocks_per_source)
                pl.when(inside)(lambda x_ref=x_ref: load(x_ref))

        def flip():
            held[:, :, :lanes] = jnp.swapaxes(held[:, :, :lanes], 1, 2)
            held[:, :, lanes:] = jnp.swapaxes(held[:, :, lanes:], 1, 2)

        def one_gate(position, carry):
            pl.when(flip_ref[segment, position] == 1)(flip)
            matrix = diagonal[position]
            flat = held[...].reshape(half * wide, pair)
            out = lax.dot_general(
                flat, matrix, (((1,), (1,)), ((), ())), preferred_element_type=jnp.float32
            )
            held[...] = out.astype(jnp.bfloat16).reshape(half, wide, pair)
            return carry

        lax.fori_loop(0, GATES, one_gate, 0)
        pl.when(flip_ref[segment, GATES] == 1)(flip)

        first = held[:, :, :lanes]
        second = held[:, :, lanes:]
        if slab_out:
            o_ref[:half] = first
            o_ref[half:] = second
        else:
            o_ref[:, :half, :] = jnp.swapaxes(first, 0, 1)
            o_ref[:, half:, :] = jnp.swapaxes(second, 0, 1)

    return kernel


def run_segment(sources, gate_mats, order, flips, segment, slab_in, slab_out, slabs, offset=0,
                into=None, out_offset=0, out_slabs=None):
    wide = gate_mats.shape[1]
    lanes = sources[0].shape[2]
    blocks = slabs // BLOCK
    per_source = blocks // len(sources)

    def source_spec(index):
        def pick(i, o, f):
            local = jnp.clip(i - index * per_source, 0, per_source - 1) + offset
            return (local, 0, 0) if slab_in else (0, local, 0)

        shape = (BLOCK, wide, lanes) if slab_in else (wide, BLOCK, lanes)
        return pl.BlockSpec(shape, pick)

    if slab_out:
        out_spec = pl.BlockSpec((BLOCK, wide, lanes), lambda i, o, f: (i + out_offset, 0, 0))
        out_shape = (out_slabs or slabs, wide, lanes)
    else:
        out_spec = pl.BlockSpec((wide, BLOCK, lanes), lambda i, o, f: (0, i, 0))
        out_shape = (wide, slabs, lanes)
    grid_spec = pltpu.PrefetchScalarGridSpec(
        num_scalar_prefetch=2,
        grid=(blocks,),
        in_specs=[pl.BlockSpec(gate_mats.shape, lambda i, o, f: (0, 0, 0))]
        + [source_spec(index) for index in range(len(sources))]
        + ([] if into is None else [pl.BlockSpec(memory_space=pl.ANY)]),
        out_specs=out_spec,
        scratch_shapes=[
            pltpu.VMEM((BLOCK // 2, wide, 2 * lanes), jnp.bfloat16),
            pltpu.VMEM((GATES, 2 * wide, 2 * lanes), jnp.bfloat16),
        ],
    )
    return pl.pallas_call(
        make_kernel(slab_in, slab_out, len(sources), per_source, segment),
        grid_spec=grid_spec,
        out_shape=jax.ShapeDtypeStruct(out_shape, sources[0].dtype),
        compiler_params=pltpu.CompilerParams(dimension_semantics=("arbitrary",)),
        input_output_aliases={} if into is None else {3 + len(sources): 0},
    )(order, flips, gate_mats, *sources, *([] if into is None else [into]))


def swap_major(values):
    amp_count = lax.axis_size("amp")
    wide, slabs, lanes = values.shape
    split = values.reshape(amp_count, wide // amp_count, slabs, lanes)
    swapped = lax.all_to_all(split, "amp", split_axis=0, concat_axis=0, tiled=True)
    return swapped.reshape(wide, slabs, lanes)


def all_sum(values, axes):
    count = lax.axis_size(axes)
    pieces = values.reshape(count, -1, 128).astype(jnp.bfloat16)
    gathered = lax.all_to_all(pieces, axes, split_axis=0, concat_axis=0, tiled=True)
    reduced = jnp.sum(gathered.astype(jnp.float32), axis=0, keepdims=True)
    spread = jnp.broadcast_to(reduced.astype(jnp.bfloat16), pieces.shape)
    whole = lax.all_to_all(spread, axes, split_axis=0, concat_axis=0, tiled=True)
    return whole.reshape(values.shape).astype(jnp.float32)


def on_device(amplitudes, adjoint, gate_mats, gate_order, gate_window, swap_window):
    slabs = amplitudes.shape[0]
    chunk = slabs // CHUNKS
    windows = gate_window.reshape(SEGS, GATES)
    starting = jnp.concatenate([jnp.zeros((1,), jnp.int32), 1 - swap_window])
    wanted = jnp.concatenate([1 - swap_window, jnp.zeros((1,), jnp.int32)])
    before = jnp.concatenate([starting[:, None], windows[:, :-1]], axis=1)
    flips = jnp.concatenate([windows != before, (windows[:, -1] != wanted)[:, None]], axis=1)
    flips = flips.astype(jnp.int32)
    order = gate_order.reshape(SEGS, GATES)
    chunks = None
    for segment in range(SEGS):
        if segment == 0:
            chunks = [
                run_segment([amplitudes], gate_mats, order, flips, segment, True, False, chunk, c * (chunk // BLOCK))
                for c in range(CHUNKS)
            ]
        elif segment < SEGS - 1:
            chunks = [run_segment([part], gate_mats, order, flips, segment, False, False, chunk) for part in chunks]
        else:
            finals = [run_segment([part], gate_mats, order, flips, segment, False, True, chunk) for part in chunks]
        if segment < SEGS - 1:
            chunks = [swap_major(part) for part in chunks]
    order = 4 * amplitudes.shape[2]
    owned_rows = order // lax.axis_size("grp")
    adjoint_flat = adjoint.reshape(-1, order)
    rows = adjoint_flat.shape[0] // CHUNKS
    partial_correlation = sum(
        lax.dot_general(
            adjoint_flat[c * rows:(c + 1) * rows], final.reshape(-1, order), (((0,), (0,)), ((), ())),
            preferred_element_type=jnp.float32,
        )
        for c, final in enumerate(finals)
    )
    current = jnp.concatenate(finals, axis=0)
    summed = all_sum(partial_correlation, ("amp", "grp"))
    owned = lax.dynamic_slice_in_dim(summed, lax.axis_index("grp") * owned_rows, owned_rows, 0)
    gram = lax.dot_general(
        summed,
        summed,
        (((0,), (0,)), ((), ())),
        precision=lax.Precision.HIGHEST,
        preferred_element_type=jnp.float32,
    )
    scale = 1.0 / jnp.sqrt(jnp.trace(gram) / order + 1e-06)
    product = jnp.dot(owned, gram, precision=lax.Precision.HIGHEST)
    environment = jnp.sqrt(jnp.float32(order)) * (
        1.5 * scale * owned - 0.5 * scale * scale * scale * product
    )
    return (current, environment)


def solution(mesh):
    in_specs = (P(("amp", "grp"), None, None), P(("amp", "grp"), None, None), P(), P(), P(), P())
    out_specs = (P(("amp", "grp"), None, None), P("grp", None))
    return jax.shard_map(
        on_device, mesh=mesh, in_specs=in_specs, out_specs=out_specs, check_vma=False
    )
```

```python
import jax
import jax.numpy as jnp
from jax import lax
from jax.experimental import pallas as pl
from jax.experimental.pallas import tpu as pltpu
from jax.sharding import PartitionSpec as P

SEGS = 4
GATES = 5
BLOCK = 32
CHUNKS = 2


def make_kernel(slab_in, slab_out, sources, blocks_per_source, segment):
    def kernel(order_ref, flip_ref, gates_ref, *refs):
        held, diagonal = refs[-2], refs[-1]
        if slab_out:
            x_refs, o_ref, flat_ref = refs[:sources], refs[-4], refs[-3]
        else:
            x_refs, o_ref = refs[:sources], refs[-3]
        half, wide, pair = held.shape
        lanes = pair // 2

        @pl.when(pl.program_id(0) == 0)
        def _():
            diagonal[...] = jnp.zeros(diagonal.shape, diagonal.dtype)
            for position in range(GATES):
                matrix = gates_ref[order_ref[segment, position]]
                diagonal[position, :lanes, :lanes] = matrix
                diagonal[position, lanes:, lanes:] = matrix

        def load(x_ref):
            if slab_in:
                slabs = x_ref[...]
            else:
                slabs = jnp.swapaxes(x_ref[...], 0, 1)
            held[:, :, :lanes] = slabs[:half]
            held[:, :, lanes:] = slabs[half:]

        if sources == 1:
            load(x_refs[0])
        else:
            step = pl.program_id(0)
            for index, x_ref in enumerate(x_refs):
                inside = (step >= index * blocks_per_source) & (step < (index + 1) * blocks_per_source)
                pl.when(inside)(lambda x_ref=x_ref: load(x_ref))

        def flip():
            held[:, :, :lanes] = jnp.swapaxes(held[:, :, :lanes], 1, 2)
            held[:, :, lanes:] = jnp.swapaxes(held[:, :, lanes:], 1, 2)

        def one_gate(position, carry):
            pl.when(flip_ref[segment, position] == 1)(flip)
            matrix = diagonal[position]
            flat = held[...].reshape(half * wide, pair)
            out = lax.dot_general(
                flat, matrix, (((1,), (1,)), ((), ())), preferred_element_type=jnp.float32
            )
            held[...] = out.astype(jnp.bfloat16).reshape(half, wide, pair)
            return carry

        lax.fori_loop(0, GATES, one_gate, 0)
        pl.when(flip_ref[segment, GATES] == 1)(flip)

        first = held[:, :, :lanes]
        second = held[:, :, lanes:]
        if slab_out:
            o_ref[:half] = first
            o_ref[half:] = second
            flat_ref[...] = o_ref[...].reshape(flat_ref.shape)
        else:
            o_ref[:, :half, :] = jnp.swapaxes(first, 0, 1)
            o_ref[:, half:, :] = jnp.swapaxes(second, 0, 1)

    return kernel


def run_segment(sources, gate_mats, order, flips, segment, slab_in, slab_out, slabs, offset=0,
                into=None, out_offset=0, out_slabs=None):
    wide = gate_mats.shape[1]
    lanes = sources[0].shape[2]
    blocks = slabs // BLOCK
    per_source = blocks // len(sources)

    def source_spec(index):
        def pick(i, o, f):
            local = jnp.clip(i - index * per_source, 0, per_source - 1) + offset
            return (local, 0, 0) if slab_in else (0, local, 0)

        shape = (BLOCK, wide, lanes) if slab_in else (wide, BLOCK, lanes)
        return pl.BlockSpec(shape, pick)

    dtype = sources[0].dtype
    if slab_out:
        rows_per_slab = wide // 4
        out_spec = [
            pl.BlockSpec((BLOCK, wide, lanes), lambda i, o, f: (i, 0, 0)),
            pl.BlockSpec((BLOCK * rows_per_slab, 4 * lanes), lambda i, o, f: (i, 0)),
        ]
        out_shape = [
            jax.ShapeDtypeStruct((slabs, wide, lanes), dtype),
            jax.ShapeDtypeStruct((slabs * rows_per_slab, 4 * lanes), dtype),
        ]
    else:
        out_spec = pl.BlockSpec((wide, BLOCK, lanes), lambda i, o, f: (0, i, 0))
        out_shape = jax.ShapeDtypeStruct((wide, slabs, lanes), dtype)
    grid_spec = pltpu.PrefetchScalarGridSpec(
        num_scalar_prefetch=2,
        grid=(blocks,),
        in_specs=[pl.BlockSpec(gate_mats.shape, lambda i, o, f: (0, 0, 0))]
        + [source_spec(index) for index in range(len(sources))]
        + ([] if into is None else [pl.BlockSpec(memory_space=pl.ANY)]),
        out_specs=out_spec,
        scratch_shapes=[
            pltpu.VMEM((BLOCK // 2, wide, 2 * lanes), jnp.bfloat16),
            pltpu.VMEM((GATES, 2 * wide, 2 * lanes), jnp.bfloat16),
        ],
    )
    return pl.pallas_call(
        make_kernel(slab_in, slab_out, len(sources), per_source, segment),
        grid_spec=grid_spec,
        out_shape=out_shape,
        compiler_params=pltpu.CompilerParams(dimension_semantics=("arbitrary",)),
        input_output_aliases={} if into is None else {3 + len(sources): 0},
    )(order, flips, gate_mats, *sources, *([] if into is None else [into]))


def swap_major(values):
    amp_count = lax.axis_size("amp")
    wide, slabs, lanes = values.shape
    split = values.reshape(amp_count, wide // amp_count, slabs, lanes)
    swapped = lax.all_to_all(split, "amp", split_axis=0, concat_axis=0, tiled=True)
    return swapped.reshape(wide, slabs, lanes)


def all_sum(values, axes):
    count = lax.axis_size(axes)
    pieces = values.reshape(count, -1, 128).astype(jnp.bfloat16)
    gathered = lax.all_to_all(pieces, axes, split_axis=0, concat_axis=0, tiled=True)
    reduced = jnp.sum(gathered.astype(jnp.float32), axis=0, keepdims=True)
    spread = jnp.broadcast_to(reduced.astype(jnp.bfloat16), pieces.shape)
    whole = lax.all_to_all(spread, axes, split_axis=0, concat_axis=0, tiled=True)
    return whole.reshape(values.shape).astype(jnp.float32)


def on_device(amplitudes, adjoint, gate_mats, gate_order, gate_window, swap_window):
    slabs = amplitudes.shape[0]
    chunk = slabs // CHUNKS
    windows = gate_window.reshape(SEGS, GATES)
    starting = jnp.concatenate([jnp.zeros((1,), jnp.int32), 1 - swap_window])
    wanted = jnp.concatenate([1 - swap_window, jnp.zeros((1,), jnp.int32)])
    before = jnp.concatenate([starting[:, None], windows[:, :-1]], axis=1)
    flips = jnp.concatenate([windows != before, (windows[:, -1] != wanted)[:, None]], axis=1)
    flips = flips.astype(jnp.int32)
    order = gate_order.reshape(SEGS, GATES)
    chunks = None
    for segment in range(SEGS):
        if segment == 0:
            chunks = [
                run_segment([amplitudes], gate_mats, order, flips, segment, True, False, chunk, c * (chunk // BLOCK))
                for c in range(CHUNKS)
            ]
        elif segment < SEGS - 1:
            chunks = [run_segment([part], gate_mats, order, flips, segment, False, False, chunk) for part in chunks]
        else:
            finals = [run_segment([part], gate_mats, order, flips, segment, False, True, chunk) for part in chunks]
        if segment < SEGS - 1:
            chunks = [swap_major(part) for part in chunks]
    order = 4 * amplitudes.shape[2]
    owned_rows = order // lax.axis_size("grp")
    adjoint_flat = adjoint.reshape(-1, order)
    rows = adjoint_flat.shape[0] // CHUNKS
    partial_correlation = sum(
        lax.dot_general(
            adjoint_flat[c * rows:(c + 1) * rows], flat, (((0,), (0,)), ((), ())),
            preferred_element_type=jnp.float32,
        )
        for c, (_, flat) in enumerate(finals)
    )
    current = jnp.concatenate([final for final, _ in finals], axis=0)
    summed = all_sum(partial_correlation, ("amp", "grp"))
    owned = lax.dynamic_slice_in_dim(summed, lax.axis_index("grp") * owned_rows, owned_rows, 0)
    gram = lax.dot_general(
        summed,
        summed,
        (((0,), (0,)), ((), ())),
        precision=lax.Precision.HIGHEST,
        preferred_element_type=jnp.float32,
    )
    scale = 1.0 / jnp.sqrt(jnp.trace(gram) / order + 1e-06)
    product = jnp.dot(owned, gram, precision=lax.Precision.HIGHEST)
    environment = jnp.sqrt(jnp.float32(order)) * (
        1.5 * scale * owned - 0.5 * scale * scale * scale * product
    )
    return (current, environment)


def solution(mesh):
    in_specs = (P(("amp", "grp"), None, None), P(("amp", "grp"), None, None), P(), P(), P(), P())
    out_specs = (P(("amp", "grp"), None, None), P("grp", None))
    return jax.shard_map(
        on_device, mesh=mesh, in_specs=in_specs, out_specs=out_specs, check_vma=False
    )
```

```python
import jax
import jax.numpy as jnp
from jax import lax
from jax.experimental import pallas as pl
from jax.experimental.pallas import tpu as pltpu
from jax.sharding import PartitionSpec as P

SEGS = 4
GATES = 5
BLOCK = 32
CHUNKS = 2


def make_kernel(slab_in, slab_out, sources, blocks_per_source, segment):
    def kernel(order_ref, flip_ref, gates_ref, *refs):
        held, diagonal = refs[-2], refs[-1]
        if slab_out:
            x_refs, adjoint_ref, o_ref, corr_ref = refs[:sources], refs[-5], refs[-4], refs[-3]
        else:
            x_refs, o_ref = refs[:sources], refs[-3]
        half, wide, pair = held.shape
        lanes = pair // 2

        @pl.when(pl.program_id(0) == 0)
        def _():
            diagonal[...] = jnp.zeros(diagonal.shape, diagonal.dtype)
            for position in range(GATES):
                matrix = gates_ref[order_ref[segment, position]]
                diagonal[position, :lanes, :lanes] = matrix
                diagonal[position, lanes:, lanes:] = matrix

        def load(x_ref):
            if slab_in:
                slabs = x_ref[...]
            else:
                slabs = jnp.swapaxes(x_ref[...], 0, 1)
            held[:, :, :lanes] = slabs[:half]
            held[:, :, lanes:] = slabs[half:]

        if sources == 1:
            load(x_refs[0])
        else:
            step = pl.program_id(0)
            for index, x_ref in enumerate(x_refs):
                inside = (step >= index * blocks_per_source) & (step < (index + 1) * blocks_per_source)
                pl.when(inside)(lambda x_ref=x_ref: load(x_ref))

        def flip():
            held[:, :, :lanes] = jnp.swapaxes(held[:, :, :lanes], 1, 2)
            held[:, :, lanes:] = jnp.swapaxes(held[:, :, lanes:], 1, 2)

        def one_gate(position, carry):
            pl.when(flip_ref[segment, position] == 1)(flip)
            matrix = diagonal[position]
            flat = held[...].reshape(half * wide, pair)
            out = lax.dot_general(
                flat, matrix, (((1,), (1,)), ((), ())), preferred_element_type=jnp.float32
            )
            held[...] = out.astype(jnp.bfloat16).reshape(half, wide, pair)
            return carry

        lax.fori_loop(0, GATES, one_gate, 0)
        pl.when(flip_ref[segment, GATES] == 1)(flip)

        first = held[:, :, :lanes]
        second = held[:, :, lanes:]
        if slab_out:
            o_ref[:half] = first
            o_ref[half:] = second
            flat = o_ref[...].reshape(adjoint_ref.shape)
            part = jnp.dot(adjoint_ref[...].T, flat, preferred_element_type=jnp.float32)

            @pl.when(pl.program_id(0) == 0)
            def _():
                corr_ref[...] = part

            @pl.when(pl.program_id(0) > 0)
            def _():
                corr_ref[...] += part
        else:
            o_ref[:, :half, :] = jnp.swapaxes(first, 0, 1)
            o_ref[:, half:, :] = jnp.swapaxes(second, 0, 1)

    return kernel


def run_segment(sources, gate_mats, order, flips, segment, slab_in, slab_out, slabs, offset=0,
                adjoint=None, adjoint_offset=0):
    wide = gate_mats.shape[1]
    lanes = sources[0].shape[2]
    blocks = slabs // BLOCK
    per_source = blocks // len(sources)

    def source_spec(index):
        def pick(i, o, f):
            local = jnp.clip(i - index * per_source, 0, per_source - 1) + offset
            return (local, 0, 0) if slab_in else (0, local, 0)

        shape = (BLOCK, wide, lanes) if slab_in else (wide, BLOCK, lanes)
        return pl.BlockSpec(shape, pick)

    dtype = sources[0].dtype
    if slab_out:
        rows_per_slab = wide // 4
        out_spec = [
            pl.BlockSpec((BLOCK, wide, lanes), lambda i, o, f: (i, 0, 0)),
            pl.BlockSpec((4 * lanes, 4 * lanes), lambda i, o, f: (0, 0)),
        ]
        out_shape = [
            jax.ShapeDtypeStruct((slabs, wide, lanes), dtype),
            jax.ShapeDtypeStruct((4 * lanes, 4 * lanes), jnp.float32),
        ]
        adjoint_spec = [pl.BlockSpec((BLOCK * rows_per_slab, 4 * lanes), lambda i, o, f: (i + adjoint_offset, 0))]
    else:
        adjoint_spec = []
    if not slab_out:
        out_spec = pl.BlockSpec((wide, BLOCK, lanes), lambda i, o, f: (0, i, 0))
        out_shape = jax.ShapeDtypeStruct((wide, slabs, lanes), dtype)
    grid_spec = pltpu.PrefetchScalarGridSpec(
        num_scalar_prefetch=2,
        grid=(blocks,),
        in_specs=[pl.BlockSpec(gate_mats.shape, lambda i, o, f: (0, 0, 0))]
        + [source_spec(index) for index in range(len(sources))]
        + adjoint_spec,
        out_specs=out_spec,
        scratch_shapes=[
            pltpu.VMEM((BLOCK // 2, wide, 2 * lanes), jnp.bfloat16),
            pltpu.VMEM((GATES, 2 * wide, 2 * lanes), jnp.bfloat16),
        ],
    )
    return pl.pallas_call(
        make_kernel(slab_in, slab_out, len(sources), per_source, segment),
        grid_spec=grid_spec,
        out_shape=out_shape,
        compiler_params=pltpu.CompilerParams(dimension_semantics=("arbitrary",)),
    )(order, flips, gate_mats, *sources, *([] if adjoint is None else [adjoint]))


def swap_major(values):
    amp_count = lax.axis_size("amp")
    wide, slabs, lanes = values.shape
    split = values.reshape(amp_count, wide // amp_count, slabs, lanes)
    swapped = lax.all_to_all(split, "amp", split_axis=0, concat_axis=0, tiled=True)
    return swapped.reshape(wide, slabs, lanes)


def all_sum(values, axes):
    count = lax.axis_size(axes)
    pieces = values.reshape(count, -1, 128).astype(jnp.bfloat16)
    gathered = lax.all_to_all(pieces, axes, split_axis=0, concat_axis=0, tiled=True)
    reduced = jnp.sum(gathered.astype(jnp.float32), axis=0, keepdims=True)
    spread = jnp.broadcast_to(reduced.astype(jnp.bfloat16), pieces.shape)
    whole = lax.all_to_all(spread, axes, split_axis=0, concat_axis=0, tiled=True)
    return whole.reshape(values.shape).astype(jnp.float32)


def on_device(amplitudes, adjoint, gate_mats, gate_order, gate_window, swap_window):
    slabs = amplitudes.shape[0]
    chunk = slabs // CHUNKS
    windows = gate_window.reshape(SEGS, GATES)
    starting = jnp.concatenate([jnp.zeros((1,), jnp.int32), 1 - swap_window])
    wanted = jnp.concatenate([1 - swap_window, jnp.zeros((1,), jnp.int32)])
    before = jnp.concatenate([starting[:, None], windows[:, :-1]], axis=1)
    flips = jnp.concatenate([windows != before, (windows[:, -1] != wanted)[:, None]], axis=1)
    flips = flips.astype(jnp.int32)
    order = gate_order.reshape(SEGS, GATES)
    chunks = None
    for segment in range(SEGS):
        if segment == 0:
            chunks = [
                run_segment([amplitudes], gate_mats, order, flips, segment, True, False, chunk, c * (chunk // BLOCK))
                for c in range(CHUNKS)
            ]
        elif segment < SEGS - 1:
            chunks = [run_segment([part], gate_mats, order, flips, segment, False, False, chunk) for part in chunks]
        else:
            adjoint_flat = adjoint.reshape(-1, 4 * adjoint.shape[2])
            finals = [
                run_segment([part], gate_mats, order, flips, segment, False, True, chunk,
                            adjoint=adjoint_flat, adjoint_offset=c * (chunk // BLOCK))
                for c, part in enumerate(chunks)
            ]
        if segment < SEGS - 1:
            chunks = [swap_major(part) for part in chunks]
    order = 4 * amplitudes.shape[2]
    owned_rows = order // lax.axis_size("grp")
    partial_correlation = sum(corr for _, corr in finals)
    current = jnp.concatenate([final for final, _ in finals], axis=0)
    summed = all_sum(partial_correlation, ("amp", "grp"))
    owned = lax.dynamic_slice_in_dim(summed, lax.axis_index("grp") * owned_rows, owned_rows, 0)
    gram = lax.dot_general(
        summed,
        summed,
        (((0,), (0,)), ((), ())),
        precision=lax.Precision.HIGHEST,
        preferred_element_type=jnp.float32,
    )
    scale = 1.0 / jnp.sqrt(jnp.trace(gram) / order + 1e-06)
    product = jnp.dot(owned, gram, precision=lax.Precision.HIGHEST)
    environment = jnp.sqrt(jnp.float32(order)) * (
        1.5 * scale * owned - 0.5 * scale * scale * scale * product
    )
    return (current, environment)


def solution(mesh):
    in_specs = (P(("amp", "grp"), None, None), P(("amp", "grp"), None, None), P(), P(), P(), P())
    out_specs = (P(("amp", "grp"), None, None), P("grp", None))
    return jax.shard_map(
        on_device, mesh=mesh, in_specs=in_specs, out_specs=out_specs, check_vma=False
    )
```

```python
import jax
import jax.numpy as jnp
from jax import lax
from jax.experimental import pallas as pl
from jax.experimental.pallas import tpu as pltpu
from jax.sharding import PartitionSpec as P

SEGS = 4
GATES = 5
BLOCK = 32
CHUNKS = 2


def make_kernel(slab_in, slab_out, sources, blocks_per_source, segment):
    def kernel(order_ref, window_ref, swap_ref, gates_ref, *refs):
        held, diagonal = refs[-2], refs[-1]
        if slab_out:
            x_refs, adjoint_ref, o_ref, corr_ref = refs[:sources], refs[-5], refs[-4], refs[-3]
        else:
            x_refs, o_ref = refs[:sources], refs[-3]
        half, wide, pair = held.shape
        lanes = pair // 2

        @pl.when(pl.program_id(0) == 0)
        def _():
            diagonal[...] = jnp.zeros(diagonal.shape, diagonal.dtype)
            for position in range(GATES):
                matrix = gates_ref[order_ref[segment * GATES + position]]
                diagonal[position, :lanes, :lanes] = matrix
                diagonal[position, lanes:, lanes:] = matrix

        def load(x_ref):
            if slab_in:
                slabs = x_ref[...]
            else:
                slabs = jnp.swapaxes(x_ref[...], 0, 1)
            held[:, :, :lanes] = slabs[:half]
            held[:, :, lanes:] = slabs[half:]

        if sources == 1:
            load(x_refs[0])
        else:
            step = pl.program_id(0)
            for index, x_ref in enumerate(x_refs):
                inside = (step >= index * blocks_per_source) & (step < (index + 1) * blocks_per_source)
                pl.when(inside)(lambda x_ref=x_ref: load(x_ref))

        def flip():
            held[:, :, :lanes] = jnp.swapaxes(held[:, :, :lanes], 1, 2)
            held[:, :, lanes:] = jnp.swapaxes(held[:, :, lanes:], 1, 2)

        starting = 0 if segment == 0 else 1 - swap_ref[segment - 1]
        wanted = 1 - swap_ref[segment] if segment < SEGS - 1 else 0

        def one_gate(position, carry):
            base = segment * GATES
            previous = window_ref[base + jnp.maximum(position - 1, 0)]
            lanes_now = jnp.where(position == 0, starting, previous)
            pl.when(window_ref[base + position] != lanes_now)(flip)
            matrix = diagonal[position]
            flat = held[...].reshape(half * wide, pair)
            out = lax.dot_general(
                flat, matrix, (((1,), (1,)), ((), ())), preferred_element_type=jnp.float32
            )
            held[...] = out.astype(jnp.bfloat16).reshape(half, wide, pair)
            return carry

        lax.fori_loop(0, GATES, one_gate, 0)
        pl.when(window_ref[segment * GATES + GATES - 1] != wanted)(flip)

        first = held[:, :, :lanes]
        second = held[:, :, lanes:]
        if slab_out:
            o_ref[:half] = first
            o_ref[half:] = second
            flat = o_ref[...].reshape(adjoint_ref.shape)
            part = jnp.dot(adjoint_ref[...].T, flat, preferred_element_type=jnp.float32)

            @pl.when(pl.program_id(0) == 0)
            def _():
                corr_ref[...] = part

            @pl.when(pl.program_id(0) > 0)
            def _():
                corr_ref[...] += part
        else:
            o_ref[:, :half, :] = jnp.swapaxes(first, 0, 1)
            o_ref[:, half:, :] = jnp.swapaxes(second, 0, 1)

    return kernel


def run_segment(sources, gate_mats, order, window, swaps, segment, slab_in, slab_out, slabs, offset=0,
                adjoint=None, adjoint_offset=0):
    wide = gate_mats.shape[1]
    lanes = sources[0].shape[2]
    blocks = slabs // BLOCK
    per_source = blocks // len(sources)

    def source_spec(index):
        def pick(i, o, w, s):
            local = jnp.clip(i - index * per_source, 0, per_source - 1) + offset
            return (local, 0, 0) if slab_in else (0, local, 0)

        shape = (BLOCK, wide, lanes) if slab_in else (wide, BLOCK, lanes)
        return pl.BlockSpec(shape, pick)

    dtype = sources[0].dtype
    if slab_out:
        rows_per_slab = wide // 4
        out_spec = [
            pl.BlockSpec((BLOCK, wide, lanes), lambda i, o, w, s: (i, 0, 0)),
            pl.BlockSpec((4 * lanes, 4 * lanes), lambda i, o, w, s: (0, 0)),
        ]
        out_shape = [
            jax.ShapeDtypeStruct((slabs, wide, lanes), dtype),
            jax.ShapeDtypeStruct((4 * lanes, 4 * lanes), jnp.float32),
        ]
        adjoint_spec = [pl.BlockSpec((BLOCK * rows_per_slab, 4 * lanes), lambda i, o, w, s: (i + adjoint_offset, 0))]
    else:
        adjoint_spec = []
    if not slab_out:
        out_spec = pl.BlockSpec((wide, BLOCK, lanes), lambda i, o, w, s: (0, i, 0))
        out_shape = jax.ShapeDtypeStruct((wide, slabs, lanes), dtype)
    grid_spec = pltpu.PrefetchScalarGridSpec(
        num_scalar_prefetch=3,
        grid=(blocks,),
        in_specs=[pl.BlockSpec(gate_mats.shape, lambda i, o, w, s: (0, 0, 0))]
        + [source_spec(index) for index in range(len(sources))]
        + adjoint_spec,
        out_specs=out_spec,
        scratch_shapes=[
            pltpu.VMEM((BLOCK // 2, wide, 2 * lanes), jnp.bfloat16),
            pltpu.VMEM((GATES, 2 * wide, 2 * lanes), jnp.bfloat16),
        ],
    )
    return pl.pallas_call(
        make_kernel(slab_in, slab_out, len(sources), per_source, segment),
        grid_spec=grid_spec,
        out_shape=out_shape,
        compiler_params=pltpu.CompilerParams(dimension_semantics=("arbitrary",)),
    )(order, window, swaps, gate_mats, *sources, *([] if adjoint is None else [adjoint]))


def swap_major(values):
    amp_count = lax.axis_size("amp")
    wide, slabs, lanes = values.shape
    split = values.reshape(amp_count, wide // amp_count, slabs, lanes)
    swapped = lax.all_to_all(split, "amp", split_axis=0, concat_axis=0, tiled=True)
    return swapped.reshape(wide, slabs, lanes)


def all_sum(values, axes):
    count = lax.axis_size(axes)
    pieces = values.reshape(count, -1, 128).astype(jnp.bfloat16)
    gathered = lax.all_to_all(pieces, axes, split_axis=0, concat_axis=0, tiled=True)
    reduced = jnp.sum(gathered.astype(jnp.float32), axis=0, keepdims=True)
    spread = jnp.broadcast_to(reduced.astype(jnp.bfloat16), pieces.shape)
    whole = lax.all_to_all(spread, axes, split_axis=0, concat_axis=0, tiled=True)
    return whole.reshape(values.shape).astype(jnp.float32)


def on_device(amplitudes, adjoint, gate_mats, gate_order, gate_window, swap_window):
    slabs = amplitudes.shape[0]
    chunk = slabs // CHUNKS
    order, window, swaps = gate_order, gate_window, swap_window
    chunks = None
    for segment in range(SEGS):
        if segment == 0:
            chunks = [
                run_segment([amplitudes], gate_mats, order, window, swaps, segment, True, False, chunk, c * (chunk // BLOCK))
                for c in range(CHUNKS)
            ]
        elif segment < SEGS - 1:
            chunks = [run_segment([part], gate_mats, order, window, swaps, segment, False, False, chunk) for part in chunks]
        else:
            adjoint_flat = adjoint.reshape(-1, 4 * adjoint.shape[2])
            finals = [
                run_segment([part], gate_mats, order, window, swaps, segment, False, True, chunk,
                            adjoint=adjoint_flat, adjoint_offset=c * (chunk // BLOCK))
                for c, part in enumerate(chunks)
            ]
        if segment < SEGS - 1:
            chunks = [swap_major(part) for part in chunks]
    order = 4 * amplitudes.shape[2]
    owned_rows = order // lax.axis_size("grp")
    partial_correlation = sum(corr for _, corr in finals)
    current = jnp.concatenate([final for final, _ in finals], axis=0)
    summed = all_sum(partial_correlation, ("amp", "grp"))
    owned = lax.dynamic_slice_in_dim(summed, lax.axis_index("grp") * owned_rows, owned_rows, 0)
    gram = lax.dot_general(
        summed,
        summed,
        (((0,), (0,)), ((), ())),
        precision=lax.Precision.HIGHEST,
        preferred_element_type=jnp.float32,
    )
    scale = 1.0 / jnp.sqrt(jnp.trace(gram) / order + 1e-06)
    product = jnp.dot(owned, gram, precision=lax.Precision.HIGHEST)
    environment = jnp.sqrt(jnp.float32(order)) * (
        1.5 * scale * owned - 0.5 * scale * scale * scale * product
    )
    return (current, environment)


def solution(mesh):
    in_specs = (P(("amp", "grp"), None, None), P(("amp", "grp"), None, None), P(), P(), P(), P())
    out_specs = (P(("amp", "grp"), None, None), P("grp", None))
    return jax.shard_map(
        on_device, mesh=mesh, in_specs=in_specs, out_specs=out_specs, check_vma=False
    )
```

```python
import jax
import jax.numpy as jnp
from jax import lax
from jax.experimental import pallas as pl
from jax.experimental.pallas import tpu as pltpu
from jax.sharding import PartitionSpec as P

SEGS = 4
GATES = 5
BLOCK = 32
LAST_BLOCK = 16
CHUNKS = 2


def make_kernel(slab_in, slab_out, sources, blocks_per_source, segment):
    def kernel(order_ref, window_ref, swap_ref, gates_ref, *refs):
        held, diagonal = refs[-2], refs[-1]
        if slab_out:
            x_refs, adjoint_ref, o_ref, corr_ref = refs[:sources], refs[-5], refs[-4], refs[-3]
        else:
            x_refs, o_ref = refs[:sources], refs[-3]
        half, wide, pair = held.shape
        lanes = pair // 2

        @pl.when(pl.program_id(0) == 0)
        def _():
            diagonal[...] = jnp.zeros(diagonal.shape, diagonal.dtype)
            for position in range(GATES):
                matrix = gates_ref[order_ref[segment * GATES + position]]
                diagonal[position, :lanes, :lanes] = matrix
                diagonal[position, lanes:, lanes:] = matrix

        def load(x_ref):
            if slab_in:
                slabs = x_ref[...]
            else:
                slabs = jnp.swapaxes(x_ref[...], 0, 1)
            held[:, :, :lanes] = slabs[:half]
            held[:, :, lanes:] = slabs[half:]

        if sources == 1:
            load(x_refs[0])
        else:
            step = pl.program_id(0)
            for index, x_ref in enumerate(x_refs):
                inside = (step >= index * blocks_per_source) & (step < (index + 1) * blocks_per_source)
                pl.when(inside)(lambda x_ref=x_ref: load(x_ref))

        def flip():
            held[:, :, :lanes] = jnp.swapaxes(held[:, :, :lanes], 1, 2)
            held[:, :, lanes:] = jnp.swapaxes(held[:, :, lanes:], 1, 2)

        starting = 0 if segment == 0 else 1 - swap_ref[segment - 1]
        wanted = 1 - swap_ref[segment] if segment < SEGS - 1 else 0

        def one_gate(position, carry):
            base = segment * GATES
            previous = window_ref[base + jnp.maximum(position - 1, 0)]
            lanes_now = jnp.where(position == 0, starting, previous)
            pl.when(window_ref[base + position] != lanes_now)(flip)
            matrix = diagonal[position]
            flat = held[...].reshape(half * wide, pair)
            out = lax.dot_general(
                flat, matrix, (((1,), (1,)), ((), ())), preferred_element_type=jnp.float32
            )
            held[...] = out.astype(jnp.bfloat16).reshape(half, wide, pair)
            return carry

        lax.fori_loop(0, GATES, one_gate, 0)
        pl.when(window_ref[segment * GATES + GATES - 1] != wanted)(flip)

        first = held[:, :, :lanes]
        second = held[:, :, lanes:]
        if slab_out:
            o_ref[:half] = first
            o_ref[half:] = second
            flat = o_ref[...].reshape(adjoint_ref.shape)
            part = jnp.dot(adjoint_ref[...].T, flat, preferred_element_type=jnp.float32)

            @pl.when(pl.program_id(0) == 0)
            def _():
                corr_ref[...] = part

            @pl.when(pl.program_id(0) > 0)
            def _():
                corr_ref[...] += part
        else:
            o_ref[:, :half, :] = jnp.swapaxes(first, 0, 1)
            o_ref[:, half:, :] = jnp.swapaxes(second, 0, 1)

    return kernel


def run_segment(sources, gate_mats, order, window, swaps, segment, slab_in, slab_out, slabs, offset=0,
                adjoint=None, adjoint_offset=0):
    BLOCK = LAST_BLOCK if slab_out else globals()["BLOCK"]
    wide = gate_mats.shape[1]
    lanes = sources[0].shape[2]
    blocks = slabs // BLOCK
    per_source = blocks // len(sources)

    def source_spec(index):
        def pick(i, o, w, s):
            local = jnp.clip(i - index * per_source, 0, per_source - 1) + offset
            return (local, 0, 0) if slab_in else (0, local, 0)

        shape = (BLOCK, wide, lanes) if slab_in else (wide, BLOCK, lanes)
        return pl.BlockSpec(shape, pick)

    dtype = sources[0].dtype
    if slab_out:
        rows_per_slab = wide // 4
        out_spec = [
            pl.BlockSpec((BLOCK, wide, lanes), lambda i, o, w, s: (i, 0, 0)),
            pl.BlockSpec((4 * lanes, 4 * lanes), lambda i, o, w, s: (0, 0)),
        ]
        out_shape = [
            jax.ShapeDtypeStruct((slabs, wide, lanes), dtype),
            jax.ShapeDtypeStruct((4 * lanes, 4 * lanes), jnp.float32),
        ]
        adjoint_spec = [pl.BlockSpec((BLOCK * rows_per_slab, 4 * lanes), lambda i, o, w, s: (i + adjoint_offset, 0))]
    else:
        adjoint_spec = []
    if not slab_out:
        out_spec = pl.BlockSpec((wide, BLOCK, lanes), lambda i, o, w, s: (0, i, 0))
        out_shape = jax.ShapeDtypeStruct((wide, slabs, lanes), dtype)
    grid_spec = pltpu.PrefetchScalarGridSpec(
        num_scalar_prefetch=3,
        grid=(blocks,),
        in_specs=[pl.BlockSpec(gate_mats.shape, lambda i, o, w, s: (0, 0, 0))]
        + [source_spec(index) for index in range(len(sources))]
        + adjoint_spec,
        out_specs=out_spec,
        scratch_shapes=[
            pltpu.VMEM((BLOCK // 2, wide, 2 * lanes), jnp.bfloat16),
            pltpu.VMEM((GATES, 2 * wide, 2 * lanes), jnp.bfloat16),
        ],
    )
    return pl.pallas_call(
        make_kernel(slab_in, slab_out, len(sources), per_source, segment),
        grid_spec=grid_spec,
        out_shape=out_shape,
        compiler_params=pltpu.CompilerParams(dimension_semantics=("arbitrary",)),
    )(order, window, swaps, gate_mats, *sources, *([] if adjoint is None else [adjoint]))


def swap_major(values):
    amp_count = lax.axis_size("amp")
    wide, slabs, lanes = values.shape
    split = values.reshape(amp_count, wide // amp_count, slabs, lanes)
    swapped = lax.all_to_all(split, "amp", split_axis=0, concat_axis=0, tiled=True)
    return swapped.reshape(wide, slabs, lanes)


def all_sum(values, axes):
    count = lax.axis_size(axes)
    pieces = values.reshape(count, -1, 128).astype(jnp.bfloat16)
    gathered = lax.all_to_all(pieces, axes, split_axis=0, concat_axis=0, tiled=True)
    reduced = jnp.sum(gathered.astype(jnp.float32), axis=0, keepdims=True)
    spread = jnp.broadcast_to(reduced.astype(jnp.bfloat16), pieces.shape)
    whole = lax.all_to_all(spread, axes, split_axis=0, concat_axis=0, tiled=True)
    return whole.reshape(values.shape).astype(jnp.float32)


def on_device(amplitudes, adjoint, gate_mats, gate_order, gate_window, swap_window):
    slabs = amplitudes.shape[0]
    chunk = slabs // CHUNKS
    order, window, swaps = gate_order, gate_window, swap_window
    chunks = None
    for segment in range(SEGS):
        if segment == 0:
            chunks = [
                run_segment([amplitudes], gate_mats, order, window, swaps, segment, True, False, chunk, c * (chunk // BLOCK))
                for c in range(CHUNKS)
            ]
        elif segment < SEGS - 1:
            chunks = [run_segment([part], gate_mats, order, window, swaps, segment, False, False, chunk) for part in chunks]
        else:
            adjoint_flat = adjoint.reshape(-1, 4 * adjoint.shape[2])
            finals = [
                run_segment([part], gate_mats, order, window, swaps, segment, False, True, chunk,
                            adjoint=adjoint_flat, adjoint_offset=c * (chunk // LAST_BLOCK))
                for c, part in enumerate(chunks)
            ]
        if segment < SEGS - 1:
            chunks = [swap_major(part) for part in chunks]
    order = 4 * amplitudes.shape[2]
    owned_rows = order // lax.axis_size("grp")
    partial_correlation = sum(corr for _, corr in finals)
    current = jnp.concatenate([final for final, _ in finals], axis=0)
    summed = all_sum(partial_correlation, ("amp", "grp"))
    owned = lax.dynamic_slice_in_dim(summed, lax.axis_index("grp") * owned_rows, owned_rows, 0)
    gram = lax.dot_general(
        summed,
        summed,
        (((0,), (0,)), ((), ())),
        precision=lax.Precision.HIGHEST,
        preferred_element_type=jnp.float32,
    )
    scale = 1.0 / jnp.sqrt(jnp.trace(gram) / order + 1e-06)
    product = jnp.dot(owned, gram, precision=lax.Precision.HIGHEST)
    environment = jnp.sqrt(jnp.float32(order)) * (
        1.5 * scale * owned - 0.5 * scale * scale * scale * product
    )
    return (current, environment)


def solution(mesh):
    in_specs = (P(("amp", "grp"), None, None), P(("amp", "grp"), None, None), P(), P(), P(), P())
    out_specs = (P(("amp", "grp"), None, None), P("grp", None))
    return jax.shard_map(
        on_device, mesh=mesh, in_specs=in_specs, out_specs=out_specs, check_vma=False
    )
```

```python
import jax
import jax.numpy as jnp
from jax import lax
from jax.experimental import pallas as pl
from jax.experimental.pallas import tpu as pltpu
from jax.sharding import PartitionSpec as P

SEGS = 4
GATES = 5
BLOCK = 32
CHUNKS = 2


def make_kernel(slab_in, slab_out, sources, blocks_per_source, segment):
    def kernel(order_ref, window_ref, swap_ref, gates_ref, *refs):
        held, diagonal = refs[-2], refs[-1]
        if slab_out:
            x_refs, adjoint_ref, o_ref, corr_ref = refs[:sources], refs[-5], refs[-4], refs[-3]
        else:
            x_refs, o_ref = refs[:sources], refs[-3]
        half, wide, pair = held.shape
        lanes = pair // 2

        @pl.when(pl.program_id(0) == 0)
        def _():
            diagonal[...] = jnp.zeros(diagonal.shape, diagonal.dtype)
            for position in range(GATES):
                matrix = gates_ref[order_ref[segment * GATES + position]]
                diagonal[position, :lanes, :lanes] = matrix
                diagonal[position, lanes:, lanes:] = matrix

        def load(x_ref):
            if slab_in:
                slabs = x_ref[...]
            else:
                slabs = jnp.swapaxes(x_ref[...], 0, 1)
            held[:, :, :lanes] = slabs[:half]
            held[:, :, lanes:] = slabs[half:]

        if sources == 1:
            load(x_refs[0])
        else:
            step = pl.program_id(0)
            for index, x_ref in enumerate(x_refs):
                inside = (step >= index * blocks_per_source) & (step < (index + 1) * blocks_per_source)
                pl.when(inside)(lambda x_ref=x_ref: load(x_ref))

        def flip():
            held[:, :, :lanes] = jnp.swapaxes(held[:, :, :lanes], 1, 2)
            held[:, :, lanes:] = jnp.swapaxes(held[:, :, lanes:], 1, 2)

        starting = 0 if segment == 0 else 1 - swap_ref[segment - 1]
        wanted = 1 - swap_ref[segment] if segment < SEGS - 1 else 0

        def one_gate(position, carry):
            base = segment * GATES
            previous = window_ref[base + jnp.maximum(position - 1, 0)]
            lanes_now = jnp.where(position == 0, starting, previous)
            pl.when(window_ref[base + position] != lanes_now)(flip)
            matrix = diagonal[position]
            flat = held[...].reshape(half * wide, pair)
            out = lax.dot_general(
                flat, matrix, (((1,), (1,)), ((), ())), preferred_element_type=jnp.float32
            )
            held[...] = out.astype(jnp.bfloat16).reshape(half, wide, pair)
            return carry

        lax.fori_loop(0, GATES, one_gate, 0)
        pl.when(window_ref[segment * GATES + GATES - 1] != wanted)(flip)

        first = held[:, :, :lanes]
        second = held[:, :, lanes:]
        if slab_out:
            o_ref[:half] = first
            o_ref[half:] = second
            flat = o_ref[...].reshape(adjoint_ref.shape)
            part = jnp.dot(adjoint_ref[...].T, flat, preferred_element_type=jnp.float32)

            @pl.when(pl.program_id(0) == 0)
            def _():
                corr_ref[...] = part

            @pl.when(pl.program_id(0) > 0)
            def _():
                corr_ref[...] += part
        else:
            o_ref[:, :half, :] = jnp.swapaxes(first, 0, 1)
            o_ref[:, half:, :] = jnp.swapaxes(second, 0, 1)

    return kernel


def run_segment(sources, gate_mats, order, window, swaps, segment, slab_in, slab_out, slabs, offset=0,
                adjoint=None, adjoint_offset=0):
    wide = gate_mats.shape[1]
    lanes = sources[0].shape[2]
    blocks = slabs // BLOCK
    per_source = blocks // len(sources)

    def source_spec(index):
        def pick(i, o, w, s):
            local = jnp.clip(i - index * per_source, 0, per_source - 1) + offset
            return (local, 0, 0) if slab_in else (0, local, 0)

        shape = (BLOCK, wide, lanes) if slab_in else (wide, BLOCK, lanes)
        return pl.BlockSpec(shape, pick)

    dtype = sources[0].dtype
    if slab_out:
        rows_per_slab = wide // 4
        out_spec = [
            pl.BlockSpec((BLOCK, wide, lanes), lambda i, o, w, s: (i, 0, 0)),
            pl.BlockSpec((4 * lanes, 4 * lanes), lambda i, o, w, s: (0, 0)),
        ]
        out_shape = [
            jax.ShapeDtypeStruct((slabs, wide, lanes), dtype),
            jax.ShapeDtypeStruct((4 * lanes, 4 * lanes), jnp.float32),
        ]
        adjoint_spec = [pl.BlockSpec((BLOCK * rows_per_slab, 4 * lanes), lambda i, o, w, s: (i + adjoint_offset, 0))]
    else:
        adjoint_spec = []
    if not slab_out:
        out_spec = pl.BlockSpec((wide, BLOCK, lanes), lambda i, o, w, s: (0, i, 0))
        out_shape = jax.ShapeDtypeStruct((wide, slabs, lanes), dtype)
    grid_spec = pltpu.PrefetchScalarGridSpec(
        num_scalar_prefetch=3,
        grid=(blocks,),
        in_specs=[pl.BlockSpec(gate_mats.shape, lambda i, o, w, s: (0, 0, 0))]
        + [source_spec(index) for index in range(len(sources))]
        + adjoint_spec,
        out_specs=out_spec,
        scratch_shapes=[
            pltpu.VMEM((BLOCK // 2, wide, 2 * lanes), jnp.bfloat16),
            pltpu.VMEM((GATES, 2 * wide, 2 * lanes), jnp.bfloat16),
        ],
    )
    return pl.pallas_call(
        make_kernel(slab_in, slab_out, len(sources), per_source, segment),
        grid_spec=grid_spec,
        out_shape=out_shape,
        compiler_params=pltpu.CompilerParams(dimension_semantics=("arbitrary",)),
    )(order, window, swaps, gate_mats, *sources, *([] if adjoint is None else [adjoint]))


def swap_major(values):
    amp_count = lax.axis_size("amp")
    wide, slabs, lanes = values.shape
    split = values.reshape(amp_count, wide // amp_count, slabs, lanes)
    swapped = lax.all_to_all(split, "amp", split_axis=0, concat_axis=0, tiled=True)
    return swapped.reshape(wide, slabs, lanes)


def all_sum(values, axes):
    count = lax.axis_size(axes)
    pieces = values.reshape(count, -1, 128).astype(jnp.bfloat16)
    gathered = lax.all_to_all(pieces, axes, split_axis=0, concat_axis=0, tiled=True)
    reduced = jnp.sum(gathered.astype(jnp.float32), axis=0, keepdims=True)
    spread = jnp.broadcast_to(reduced.astype(jnp.bfloat16), pieces.shape)
    whole = lax.all_to_all(spread, axes, split_axis=0, concat_axis=0, tiled=True)
    return whole.reshape(values.shape).astype(jnp.float32)


def on_device(amplitudes, adjoint, gate_mats, gate_order, gate_window, swap_window):
    slabs = amplitudes.shape[0]
    chunk = slabs // CHUNKS
    order, window, swaps = gate_order, gate_window, swap_window
    chunks = None
    for segment in range(SEGS):
        if segment == 0:
            chunks = [
                run_segment([amplitudes], gate_mats, order, window, swaps, segment, True, False, chunk, c * (chunk // BLOCK))
                for c in range(CHUNKS)
            ]
        elif segment < SEGS - 1:
            chunks = [run_segment([part], gate_mats, order, window, swaps, segment, False, False, chunk) for part in chunks]
        else:
            adjoint_flat = adjoint.reshape(-1, 4 * adjoint.shape[2])
            finals = [
                run_segment([part], gate_mats, order, window, swaps, segment, False, True, chunk,
                            adjoint=adjoint_flat, adjoint_offset=c * (chunk // BLOCK))
                for c, part in enumerate(chunks)
            ]
        if segment < SEGS - 1:
            chunks = [swap_major(part) for part in chunks]
    order = 4 * amplitudes.shape[2]
    owned_rows = order // lax.axis_size("grp")
    partial_correlation = sum(corr for _, corr in finals)
    current = jnp.concatenate([final for final, _ in finals], axis=0)
    summed = all_sum(partial_correlation, ("amp", "grp"))
    owned = lax.dynamic_slice_in_dim(summed, lax.axis_index("grp") * owned_rows, owned_rows, 0)
    gram = lax.dot_general(
        summed,
        summed,
        (((0,), (0,)), ((), ())),
        precision=lax.Precision.HIGH,
        preferred_element_type=jnp.float32,
    )
    scale = 1.0 / jnp.sqrt(jnp.trace(gram) / order + 1e-06)
    product = jnp.dot(owned, gram, precision=lax.Precision.HIGH)
    environment = jnp.sqrt(jnp.float32(order)) * (
        1.5 * scale * owned - 0.5 * scale * scale * scale * product
    )
    return (current, environment)


def solution(mesh):
    in_specs = (P(("amp", "grp"), None, None), P(("amp", "grp"), None, None), P(), P(), P(), P())
    out_specs = (P(("amp", "grp"), None, None), P("grp", None))
    return jax.shard_map(
        on_device, mesh=mesh, in_specs=in_specs, out_specs=out_specs, check_vma=False
    )
```
